32 devices in a mesh: parts: 2 (over y), fsdp: 4 (over z), seq: 2 (over x), ctx: 2 (over core).
Axes of the slice: x: 2, y: 2, z: 4, core: 2. Of those that a mesh axis runs over, the one named last changes fastest.
Arguments:
- hidden_in: bfloat16 [8, 2, 96, 8192], P(('parts', 'fsdp'), 'ctx', None, 'seq'), parts along dimension 0, may hold values from -6 to 6
- weight: bfloat16 [8192, 4096], P('fsdp', 'seq'), may hold values from -0.0625 to 0.0625
- clip_upper: float32 [128, 4096], P(('parts', 'fsdp'), 'seq'), parts along dimension 0, may hold values from 0.5 to 3
- clip_lower: float32 [128, 4096], P(('parts', 'fsdp'), 'seq'), parts along dimension 0, may hold values from -0.5 to 2.5
- filters: float32 [256, 7], P('seq'), may hold values from -3 to 3
- gate: bfloat16 [8, 2, 96, 4096], P(('parts', 'fsdp'), 'ctx', None, 'seq'), parts along dimension 0, may hold values from -6 to 6
- target: bfloat16 [8, 2, 96, 4096], P(('parts', 'fsdp'), 'ctx', None, 'seq'), parts along dimension 0, may hold values from -6 to 6
Outputs:
- grad_upper: float32 [128, 4096], P(('parts', 'fsdp'), 'seq'), parts along dimension 0
- grad_lower: float32 [128, 4096], P(('parts', 'fsdp'), 'seq'), parts along dimension 0
The draws below stay inside these ranges and needn't reach their ends.
There are 2 independent parts, one for each index of `parts`. The reference program is written for one: setup_inputs(seed, part) draws one part's arguments, and reference() takes and returns one part's arrays. A program takes and returns all parts, laid end to end along the dimension named above; an argument that names none is the same for every part. Nothing has to cross between parts.
All inputs are finite; a program needn't handle non-finite values.
Results may differ from the reference program's by a relative error of at most 0.0039.
Values may be sent and summed in bfloat16 or wider, within the bound.
No kernel may reach another device: no remote copies, remote signals or barrier semaphores. Data moves between devices by JAX's collectives and lax.ppermute only.
A program may use at most 128 MiB of HBM per device.

```python
import jax
import jax.numpy as jnp
from jax import lax

D = 8192
DOUT = 4096
FILT = 7
CGROUP = 16
SPAN = 96
SPANS = 2
SEQS = 4
GROUPS = 64
FGROUPS = 256


def level_of(own_key, shape, pieces, least, largest):
    gain = 1.0
    for axis_at, shards_of in pieces:
        heights = jax.random.uniform(jax.random.fold_in(jax.random.fold_in(own_key, 6), axis_at), (shards_of,), jnp.float32, least / len(pieces), largest / len(pieces))
        gain = gain * jnp.repeat(jnp.exp(heights), shape[axis_at] // shards_of).reshape((-1,) + (1,) * (len(shape) - 1 - axis_at))
    return gain


def normal_values(stream_key, extent, deviation, most, pieces=(), dtype=jnp.bfloat16):
    level = level_of(stream_key, extent, pieces, -0.22, 0.18) if pieces else 1.0
    drawn = jax.random.normal(stream_key, extent, jnp.float32) * deviation * level
    return jnp.minimum(jnp.maximum(drawn, -most), most).astype(dtype)


def setup_inputs(seed: int = 0, part: int = 0) -> dict:
    keys = jax.random.split(jax.random.key(seed), 8)
    part_splits = jax.random.split(jax.random.fold_in(keys[7], part), 8)
    hidden_in = normal_values(part_splits[0], (SEQS, SPANS, SPAN, D), 1.0, 6.0, ((0, 4), (1, 2), (3, 2)))
    weight = normal_values(keys[1], (D, DOUT), D ** -0.5, 0.0625, ((0, 4), (1, 2)))
    clip_upper = jnp.clip(0.5 + 2.5 * jax.random.uniform(part_splits[2], (GROUPS, DOUT), jnp.float32) ** level_of(part_splits[2], (GROUPS, DOUT), ((0, 4), (1, 2)), -0.2, 0.2), 0.5, 3.0)
    clip_lower = jnp.clip(-0.5 + 3.0 * jax.random.uniform(part_splits[3], (GROUPS, DOUT), jnp.float32) ** level_of(part_splits[3], (GROUPS, DOUT), ((0, 4), (1, 2)), -0.2, 0.2), -0.5, 2.5)
    filters = normal_values(keys[4], (FGROUPS, FILT), 0.5, 3.0, ((0, 2),), jnp.float32)
    gate = normal_values(part_splits[5], (SEQS, SPANS, SPAN, DOUT), 1.0, 6.0, ((0, 4), (1, 2), (3, 2)))
    target = normal_values(part_splits[6], (SEQS, SPANS, SPAN, DOUT), 1.0, 6.0, ((0, 4), (1, 2), (3, 2)))
    return {"hidden_in": hidden_in, "weight": weight, "clip_upper": clip_upper, "clip_lower": clip_lower, "filters": filters, "gate": gate, "target": target}


def soft_clip(values, upper_logit, lower_logit):
    rows = values.shape[0]
    groups = upper_logit.shape[0]
    blocks = values.reshape(groups, rows // groups, values.shape[1])
    amax = lax.optimization_barrier(jnp.max(jnp.abs(blocks), axis=1)) + 1e-06
    upper = jax.nn.sigmoid(upper_logit) * amax
    lower = -jax.nn.sigmoid(lower_logit) * amax
    center = ((upper + lower) * 0.5)[:, None, :]
    radius = ((upper - lower) * 0.5)[:, None, :]
    clipped = center + radius * jnp.tanh((blocks - center) / radius)
    return clipped.reshape(rows, values.shape[1])

def reference(hidden_in, weight, clip_upper, clip_lower, filters, gate, target):
    length = SPANS * SPAN
    wvals = weight.astype(jnp.float32)
    clipped_b = soft_clip(wvals, clip_upper, clip_lower).astype(jnp.bfloat16)
    taps = jnp.repeat(filters, CGROUP, axis=0).T
    scale = 1024.0 / jnp.sqrt(jnp.float32(SEQS * SPANS * SPAN))
    pad = FILT - 1

    def one_sequence(total, index):
        rows = hidden_in[index].reshape(length, D)
        gates = gate[index].reshape(length, DOUT).astype(jnp.float32)
        wanted = target[index].reshape(length, DOUT).astype(jnp.float32)
        proj = jnp.dot(rows, clipped_b, preferred_element_type=jnp.float32).astype(jnp.bfloat16)
        padded = jnp.concatenate([jnp.zeros((pad, DOUT), jnp.float32), proj.astype(jnp.float32)], axis=0)
        conv = jnp.zeros((length, DOUT), jnp.float32)
        for tap in range(FILT):
            conv = conv + taps[tap] * padded[pad - tap:pad - tap + length]
        out = gates * conv
        d_conv = scale * (out - wanted) * gates
        padded_back = jnp.concatenate([d_conv, jnp.zeros((pad, DOUT), jnp.float32)], axis=0)
        d_proj = jnp.zeros((length, DOUT), jnp.float32)
        for tap in range(FILT):
            d_proj = d_proj + taps[tap] * padded_back[tap:tap + length]
        d_proj = d_proj.astype(jnp.bfloat16)
        contrib = lax.dot_general(rows, d_proj, (((0,), (0,)), ((), ())), preferred_element_type=jnp.float32)
        return (total + contrib, None)
    d_clipped, _ = lax.scan(one_sequence, jnp.zeros((D, DOUT), jnp.float32), jnp.arange(SEQS))
    _, pull = jax.vjp(lambda upper_logit, lower_logit: soft_clip(wvals, upper_logit, lower_logit), clip_upper, clip_lower)
    grad_upper, grad_lower = pull(d_clipped)
    return (grad_upper, grad_lower)
```

```python
import jax
import jax.numpy as jnp
from jax import lax
from jax.sharding import PartitionSpec as P

FILT = 7
CGROUP = 16


def from_behind(value, axis, by):
    devices = lax.axis_size(axis)
    pairs = [(i, i + by) for i in range(devices) if 0 <= i + by < devices]
    return lax.ppermute(value, axis, pairs)


def soft_clip(values, upper_logit, lower_logit):
    rows = values.shape[0]
    groups = upper_logit.shape[0]
    blocks = values.reshape(groups, rows // groups, values.shape[1])
    amax = jnp.max(jnp.abs(blocks), axis=1) + 1e-06
    upper = jax.nn.sigmoid(upper_logit) * amax
    lower = -jax.nn.sigmoid(lower_logit) * amax
    center = ((upper + lower) * 0.5)[:, None, :]
    radius = ((upper - lower) * 0.5)[:, None, :]
    clipped = center + radius * jnp.tanh((blocks - center) / radius)
    return clipped.reshape(rows, values.shape[1])


def on_device(hidden_in, weight, clip_upper, clip_lower, filters, gate, target):
    shards = lax.axis_size("fsdp")
    width = hidden_in.shape[-1]
    local_rows = hidden_in.reshape(-1, width)
    length = local_rows.shape[0]
    rows, columns = weight.shape
    features = lax.all_gather(local_rows, "seq", axis=1, tiled=True)
    pieces = features.reshape(length, shards, rows).transpose(1, 0, 2)
    mine = lax.all_to_all(pieces, "fsdp", 0, 0)
    inputs = mine.reshape(shards * length, rows)

    values = weight.astype(jnp.float32)
    quant = soft_clip(values, clip_upper, clip_lower).astype(jnp.bfloat16)
    partial = jnp.dot(inputs, quant, preferred_element_type=jnp.float32)
    proj = lax.psum_scatter(partial, "fsdp", scatter_dimension=0, tiled=True).astype(jnp.bfloat16)

    taps = jnp.repeat(filters, CGROUP, axis=0).T
    pad = FILT - 1
    previous = from_behind(proj[length - pad :], "ctx", 1)
    padded = jnp.concatenate([previous, proj], axis=0).astype(jnp.float32)
    conv = jnp.zeros((length, columns), jnp.float32)
    for tap in range(FILT):
        conv = conv + taps[tap] * padded[pad - tap : pad - tap + length]
    gates = gate.reshape(length, columns).astype(jnp.float32)
    wanted = target.reshape(length, columns).astype(jnp.float32)
    total_tokens = lax.axis_size("fsdp") * lax.axis_size("ctx") * length
    scale = 1024.0 / jnp.sqrt(jnp.float32(total_tokens))
    d_conv = scale * (gates * conv - wanted) * gates
    following = from_behind(d_conv[:pad], "ctx", -1)
    padded_back = jnp.concatenate([d_conv, following], axis=0)
    d_proj = jnp.zeros((length, columns), jnp.float32)
    for tap in range(FILT):
        d_proj = d_proj + taps[tap] * padded_back[tap : tap + length]
    d_proj = d_proj.astype(jnp.bfloat16)

    d_all = lax.all_gather(d_proj, "fsdp", axis=0, tiled=True)
    d_clipped = lax.dot_general(
        inputs, d_all, (((0,), (0,)), ((), ())), preferred_element_type=jnp.float32
    )
    _, pull = jax.vjp(
        lambda upper_logit, lower_logit: soft_clip(values, upper_logit, lower_logit),
        clip_upper,
        clip_lower,
    )
    grad_up, grad_low = pull(d_clipped)
    grad_upper, grad_lower = lax.psum((grad_up, grad_low), "ctx")
    return (grad_upper, grad_lower)


def solution(mesh):
    return jax.shard_map(
        on_device,
        mesh=mesh,
        in_specs=(
            P(("parts", "fsdp"), "ctx", None, "seq"),
            P("fsdp", "seq"),
            P(("parts", "fsdp"), "seq"),
            P(("parts", "fsdp"), "seq"),
            P("seq", None),
            P(("parts", "fsdp"), "ctx", None, "seq"),
            P(("parts", "fsdp"), "ctx", None, "seq"),
        ),
        out_specs=(P(("parts", "fsdp"), "seq"), P(("parts", "fsdp"), "seq")),
        check_vma=False,
    )
```

```python
import jax
import jax.numpy as jnp
from jax import lax
from jax.sharding import PartitionSpec as P

FILT = 7
CGROUP = 16


def from_behind(value, axis, by):
    devices = lax.axis_size(axis)
    pairs = [(i, i + by) for i in range(devices) if 0 <= i + by < devices]
    return lax.ppermute(value, axis, pairs)


def soft_clip(values, upper_logit, lower_logit):
    rows = values.shape[0]
    groups = upper_logit.shape[0]
    blocks = values.reshape(groups, rows // groups, values.shape[1])
    amax = jnp.max(jnp.abs(blocks), axis=1) + 1e-06
    upper = jax.nn.sigmoid(upper_logit) * amax
    lower = -jax.nn.sigmoid(lower_logit) * amax
    center = ((upper + lower) * 0.5)[:, None, :]
    radius = ((upper - lower) * 0.5)[:, None, :]
    clipped = center + radius * jnp.tanh((blocks - center) / radius)
    return clipped.reshape(rows, values.shape[1])


def gather_features(local_rows):
    devices = lax.axis_size("seq")
    if devices != 2:
        return lax.all_gather(local_rows, "seq", axis=1, tiled=True)
    other = lax.ppermute(local_rows, "seq", [(0, 1), (1, 0)])
    first = lax.axis_index("seq") == 0
    return jnp.where(
        first,
        jnp.concatenate([local_rows, other], axis=1),
        jnp.concatenate([other, local_rows], axis=1),
    )


def sum_over_ctx(value):
    devices = lax.axis_size("ctx")
    if devices != 2:
        return lax.psum(value, "ctx")
    return value + lax.ppermute(value, "ctx", [(0, 1), (1, 0)])


def on_device(hidden_in, weight, clip_upper, clip_lower, filters, gate, target):
    shards = lax.axis_size("fsdp")
    width = hidden_in.shape[-1]
    local_rows = hidden_in.reshape(-1, width)
    length = local_rows.shape[0]
    rows, columns = weight.shape
    features = gather_features(local_rows)
    pieces = features.reshape(length, shards, rows).transpose(1, 0, 2)
    mine = lax.all_to_all(pieces, "fsdp", 0, 0)
    inputs = mine.reshape(shards * length, rows)

    values = weight.astype(jnp.float32)
    quant = soft_clip(values, clip_upper, clip_lower).astype(jnp.bfloat16)
    partial = jnp.dot(inputs, quant, preferred_element_type=jnp.float32)
    received = lax.all_to_all(partial.reshape(shards, length, columns), "fsdp", 0, 0)
    proj = jnp.sum(received, axis=0).astype(jnp.bfloat16)

    taps = jnp.repeat(filters, CGROUP, axis=0).T
    pad = FILT - 1
    previous = from_behind(proj[length - pad :], "ctx", 1)
    padded = jnp.concatenate([previous, proj], axis=0).astype(jnp.float32)
    conv = jnp.zeros((length, columns), jnp.float32)
    for tap in range(FILT):
        conv = conv + taps[tap] * padded[pad - tap : pad - tap + length]
    gates = gate.reshape(length, columns).astype(jnp.float32)
    wanted = target.reshape(length, columns).astype(jnp.float32)
    total_tokens = lax.axis_size("fsdp") * lax.axis_size("ctx") * length
    scale = 1024.0 / jnp.sqrt(jnp.float32(total_tokens))
    d_conv = scale * (gates * conv - wanted) * gates
    following = from_behind(d_conv[:pad], "ctx", -1)
    padded_back = jnp.concatenate([d_conv, following], axis=0)
    d_proj = jnp.zeros((length, columns), jnp.float32)
    for tap in range(FILT):
        d_proj = d_proj + taps[tap] * padded_back[tap : tap + length]
    d_proj = d_proj.astype(jnp.bfloat16)

    copies = jnp.broadcast_to(d_proj[None], (shards, length, columns))
    d_all = lax.all_to_all(copies, "fsdp", 0, 0).reshape(shards * length, columns)
    d_clipped = lax.dot_general(
        inputs, d_all, (((0,), (0,)), ((), ())), preferred_element_type=jnp.float32
    )
    _, pull = jax.vjp(
        lambda upper_logit, lower_logit: soft_clip(values, upper_logit, lower_logit),
        clip_upper,
        clip_lower,
    )
    grad_up, grad_low = pull(d_clipped)
    grad_upper, grad_lower = sum_over_ctx(grad_up), sum_over_ctx(grad_low)
    return (grad_upper, grad_lower)


def solution(mesh):
    return jax.shard_map(
        on_device,
        mesh=mesh,
        in_specs=(
            P(("parts", "fsdp"), "ctx", None, "seq"),
            P("fsdp", "seq"),
            P(("parts", "fsdp"), "seq"),
            P(("parts", "fsdp"), "seq"),
            P("seq", None),
            P(("parts", "fsdp"), "ctx", None, "seq"),
            P(("parts", "fsdp"), "ctx", None, "seq"),
        ),
        out_specs=(P(("parts", "fsdp"), "seq"), P(("parts", "fsdp"), "seq")),
        check_vma=False,
    )
```

```python
import jax
import jax.numpy as jnp
from jax import lax
from jax.sharding import PartitionSpec as P

FILT = 7
CGROUP = 16


def from_behind(value, axis, by):
    devices = lax.axis_size(axis)
    pairs = [(i, i + by) for i in range(devices) if 0 <= i + by < devices]
    return lax.ppermute(value, axis, pairs)


def soft_clip(values, upper_logit, lower_logit):
    rows = values.shape[0]
    groups = upper_logit.shape[0]
    blocks = values.reshape(groups, rows // groups, values.shape[1])
    amax = jnp.max(jnp.abs(blocks), axis=1) + 1e-06
    upper = jax.nn.sigmoid(upper_logit) * amax
    lower = -jax.nn.sigmoid(lower_logit) * amax
    center = ((upper + lower) * 0.5)[:, None, :]
    radius = ((upper - lower) * 0.5)[:, None, :]
    clipped = center + radius * jnp.tanh((blocks - center) / radius)
    return clipped.reshape(rows, values.shape[1])


def gather_features(local_rows):
    devices = lax.axis_size("seq")
    if devices != 2:
        return lax.all_gather(local_rows, "seq", axis=1, tiled=True)
    other = lax.ppermute(local_rows, "seq", [(0, 1), (1, 0)])
    first = lax.axis_index("seq") == 0
    return jnp.where(
        first,
        jnp.concatenate([local_rows, other], axis=1),
        jnp.concatenate([other, local_rows], axis=1),
    )


def sum_over_ctx(value):
    devices = lax.axis_size("ctx")
    if devices != 2:
        return lax.psum(value, "ctx")
    return value + lax.ppermute(value, "ctx", [(0, 1), (1, 0)])


def line_reduce_scatter(partial_for, axis):
    devices = lax.axis_size(axis)
    me = lax.axis_index(axis)
    right = left = None
    for step in range(1, devices):
        term = partial_for(jnp.minimum(me + devices - step, devices - 1))
        if right is not None:
            term = right + term
        pairs = [(i, i + 1) for i in range(0, min(step - 1, devices - 2) + 1)]
        right = lax.ppermute(term, axis, pairs)
        term = partial_for(jnp.maximum(me - devices + step, 0))
        if left is not None:
            term = left + term
        pairs = [(i, i - 1) for i in range(max(devices - step, 1), devices)]
        left = lax.ppermute(term, axis, pairs)
    own = partial_for(me)
    if right is None:
        return own
    return own + right + left


def line_all_gather(value, axis):
    devices = lax.axis_size(axis)
    me = lax.axis_index(axis)
    gathered = jnp.zeros((devices,) + value.shape, value.dtype)
    gathered = lax.dynamic_update_index_in_dim(gathered, value, me, 0)
    right = left = value

    def place(gathered, block, origin):
        valid = (origin >= 0) & (origin < devices)
        at = jnp.clip(origin, 0, devices - 1)
        held = lax.dynamic_index_in_dim(gathered, at, 0, keepdims=False)
        return lax.dynamic_update_index_in_dim(gathered, jnp.where(valid, block, held), at, 0)

    for step in range(1, devices):
        right = lax.ppermute(right, axis, [(i, i + 1) for i in range(step - 1, devices - 1)])
        left = lax.ppermute(left, axis, [(i, i - 1) for i in range(1, devices - step + 1)])
        gathered = place(gathered, right, me - step)
        gathered = place(gathered, left, me + step)
    return gathered


def on_device(hidden_in, weight, clip_upper, clip_lower, filters, gate, target):
    shards = lax.axis_size("fsdp")
    width = hidden_in.shape[-1]
    local_rows = hidden_in.reshape(-1, width)
    length = local_rows.shape[0]
    rows, columns = weight.shape
    features = gather_features(local_rows)
    pieces = features.reshape(length, shards, rows).transpose(1, 0, 2)
    mine = lax.all_to_all(pieces, "fsdp", 0, 0)
    inputs = mine.reshape(shards * length, rows)

    values = weight.astype(jnp.float32)
    quant = soft_clip(values, clip_upper, clip_lower).astype(jnp.bfloat16)

    def partial_for(chunk):
        block = lax.dynamic_index_in_dim(mine, chunk, 0, keepdims=False)
        return jnp.dot(block, quant, preferred_element_type=jnp.float32)

    proj = line_reduce_scatter(partial_for, "fsdp").astype(jnp.bfloat16)

    taps = jnp.repeat(filters, CGROUP, axis=0).T
    pad = FILT - 1
    previous = from_behind(proj[length - pad :], "ctx", 1)
    padded = jnp.concatenate([previous, proj], axis=0).astype(jnp.float32)
    conv = jnp.zeros((length, columns), jnp.float32)
    for tap in range(FILT):
        conv = conv + taps[tap] * padded[pad - tap : pad - tap + length]
    gates = gate.reshape(length, columns).astype(jnp.float32)
    wanted = target.reshape(length, columns).astype(jnp.float32)
    total_tokens = lax.axis_size("fsdp") * lax.axis_size("ctx") * length
    scale = 1024.0 / jnp.sqrt(jnp.float32(total_tokens))
    d_conv = scale * (gates * conv - wanted) * gates
    following = from_behind(d_conv[:pad], "ctx", -1)
    padded_back = jnp.concatenate([d_conv, following], axis=0)
    d_proj = jnp.zeros((length, columns), jnp.float32)
    for tap in range(FILT):
        d_proj = d_proj + taps[tap] * padded_back[tap : tap + length]
    d_proj = d_proj.astype(jnp.bfloat16)

    d_all = line_all_gather(d_proj, "fsdp").reshape(shards * length, columns)
    d_clipped = lax.dot_general(
        inputs, d_all, (((0,), (0,)), ((), ())), preferred_element_type=jnp.float32
    )
    _, pull = jax.vjp(
        lambda upper_logit, lower_logit: soft_clip(values, upper_logit, lower_logit),
        clip_upper,
        clip_lower,
    )
    grad_up, grad_low = pull(d_clipped)
    grad_upper, grad_lower = sum_over_ctx(grad_up), sum_over_ctx(grad_low)
    return (grad_upper, grad_lower)


def solution(mesh):
    return jax.shard_map(
        on_device,
        mesh=mesh,
        in_specs=(
            P(("parts", "fsdp"), "ctx", None, "seq"),
            P("fsdp", "seq"),
            P(("parts", "fsdp"), "seq"),
            P(("parts", "fsdp"), "seq"),
            P("seq", None),
            P(("parts", "fsdp"), "ctx", None, "seq"),
            P(("parts", "fsdp"), "ctx", None, "seq"),
        ),
        out_specs=(P(("parts", "fsdp"), "seq"), P(("parts", "fsdp"), "seq")),
        check_vma=False,
    )
```

```python
import jax
import jax.numpy as jnp
from jax import lax
from jax.sharding import PartitionSpec as P

FILT = 7
CGROUP = 16


def from_behind(value, axis, by):
    devices = lax.axis_size(axis)
    pairs = [(i, i + by) for i in range(devices) if 0 <= i + by < devices]
    return lax.ppermute(value, axis, pairs)


def soft_clip(values, upper_logit, lower_logit):
    rows = values.shape[0]
    groups = upper_logit.shape[0]
    blocks = values.reshape(groups, rows // groups, values.shape[1])
    amax = jnp.max(jnp.abs(blocks), axis=1) + 1e-06
    upper = jax.nn.sigmoid(upper_logit) * amax
    lower = -jax.nn.sigmoid(lower_logit) * amax
    center = ((upper + lower) * 0.5)[:, None, :]
    radius = ((upper - lower) * 0.5)[:, None, :]
    clipped = center + radius * jnp.tanh((blocks - center) / radius)
    return clipped.reshape(rows, values.shape[1])


def gather_features(local_rows):
    devices = lax.axis_size("seq")
    if devices != 2:
        return lax.all_gather(local_rows, "seq", axis=1, tiled=True)
    other = lax.ppermute(local_rows, "seq", [(0, 1), (1, 0)])
    first = lax.axis_index("seq") == 0
    return jnp.where(
        first,
        jnp.concatenate([local_rows, other], axis=1),
        jnp.concatenate([other, local_rows], axis=1),
    )


def sum_over_ctx(value):
    devices = lax.axis_size("ctx")
    if devices != 2:
        return lax.psum(value, "ctx")
    return value + lax.ppermute(value, "ctx", [(0, 1), (1, 0)])


def on_device(hidden_in, weight, clip_upper, clip_lower, filters, gate, target):
    shards = lax.axis_size("fsdp")
    width = hidden_in.shape[-1]
    local_rows = hidden_in.reshape(-1, width)
    length = local_rows.shape[0]
    rows, columns = weight.shape
    features = gather_features(local_rows)
    pieces = features.reshape(length, shards, rows).transpose(1, 0, 2)
    mine = lax.all_to_all(pieces, "fsdp", 0, 0)
    inputs = mine.reshape(shards * length, rows)

    values = weight.astype(jnp.float32)
    quant = soft_clip(values, clip_upper, clip_lower).astype(jnp.bfloat16)
    partial = jnp.dot(inputs, quant, preferred_element_type=jnp.float32).reshape(shards, length, columns)
    me = lax.axis_index("fsdp")
    received = lax.all_to_all(partial.astype(jnp.float16), "fsdp", 0, 0).astype(jnp.float32)
    others = jnp.where((jnp.arange(shards) == me)[:, None, None], 0.0, received)
    own = lax.dynamic_index_in_dim(partial, me, 0, keepdims=False)
    proj = (own + jnp.sum(others, axis=0)).astype(jnp.bfloat16)

    taps = jnp.repeat(filters, CGROUP, axis=0).T
    pad = FILT - 1
    previous = from_behind(proj[length - pad :], "ctx", 1)
    padded = jnp.concatenate([previous, proj], axis=0).astype(jnp.float32)
    conv = jnp.zeros((length, columns), jnp.float32)
    for tap in range(FILT):
        conv = conv + taps[tap] * padded[pad - tap : pad - tap + length]
    gates = gate.reshape(length, columns).astype(jnp.float32)
    wanted = target.reshape(length, columns).astype(jnp.float32)
    total_tokens = lax.axis_size("fsdp") * lax.axis_size("ctx") * length
    scale = 1024.0 / jnp.sqrt(jnp.float32(total_tokens))
    d_conv = scale * (gates * conv - wanted) * gates
    following = from_behind(d_conv[:pad], "ctx", -1)
    padded_back = jnp.concatenate([d_conv, following], axis=0)
    d_proj = jnp.zeros((length, columns), jnp.float32)
    for tap in range(FILT):
        d_proj = d_proj + taps[tap] * padded_back[tap : tap + length]
    d_proj = d_proj.astype(jnp.bfloat16)

    copies = jnp.broadcast_to(d_proj[None], (shards, length, columns))
    d_all = lax.all_to_all(copies, "fsdp", 0, 0).reshape(shards * length, columns)
    d_clipped = lax.dot_general(
        inputs, d_all, (((0,), (0,)), ((), ())), preferred_element_type=jnp.float32
    )
    _, pull = jax.vjp(
        lambda upper_logit, lower_logit: soft_clip(values, upper_logit, lower_logit),
        clip_upper,
        clip_lower,
    )
    grad_up, grad_low = pull(d_clipped)
    grad_upper, grad_lower = sum_over_ctx(grad_up), sum_over_ctx(grad_low)
    return (grad_upper, grad_lower)


def solution(mesh):
    return jax.shard_map(
        on_device,
        mesh=mesh,
        in_specs=(
            P(("parts", "fsdp"), "ctx", None, "seq"),
            P("fsdp", "seq"),
            P(("parts", "fsdp"), "seq"),
            P(("parts", "fsdp"), "seq"),
            P("seq", None),
            P(("parts", "fsdp"), "ctx", None, "seq"),
            P(("parts", "fsdp"), "ctx", None, "seq"),
        ),
        out_specs=(P(("parts", "fsdp"), "seq"), P(("parts", "fsdp"), "seq")),
        check_vma=False,
    )
```

```python
import jax
import jax.numpy as jnp
from jax import lax
from jax.sharding import PartitionSpec as P

FILT = 7
CGROUP = 16


def from_behind(value, axis, by):
    devices = lax.axis_size(axis)
    pairs = [(i, i + by) for i in range(devices) if 0 <= i + by < devices]
    return lax.ppermute(value, axis, pairs)


def soft_clip(values, upper_logit, lower_logit):
    rows = values.shape[0]
    groups = upper_logit.shape[0]
    blocks = values.reshape(groups, rows // groups, values.shape[1])
    amax = jnp.max(jnp.abs(blocks), axis=1) + 1e-06
    upper = jax.nn.sigmoid(upper_logit) * amax
    lower = -jax.nn.sigmoid(lower_logit) * amax
    center = ((upper + lower) * 0.5)[:, None, :]
    radius = ((upper - lower) * 0.5)[:, None, :]
    clipped = center + radius * jnp.tanh((blocks - center) / radius)
    return clipped.reshape(rows, values.shape[1])


def gather_features(local_rows):
    devices = lax.axis_size("seq")
    if devices != 2:
        return lax.all_gather(local_rows, "seq", axis=1, tiled=True)
    other = lax.ppermute(local_rows, "seq", [(0, 1), (1, 0)])
    first = lax.axis_index("seq") == 0
    return jnp.where(
        first,
        jnp.concatenate([local_rows, other], axis=1),
        jnp.concatenate([other, local_rows], axis=1),
    )


def sum_over_ctx(value):
    devices = lax.axis_size("ctx")
    if devices != 2:
        return lax.psum(value, "ctx")
    return value + lax.ppermute(value, "ctx", [(0, 1), (1, 0)])


def on_device(hidden_in, weight, clip_upper, clip_lower, filters, gate, target):
    shards = lax.axis_size("fsdp")
    width = hidden_in.shape[-1]
    local_rows = hidden_in.reshape(-1, width)
    length = local_rows.shape[0]
    rows, columns = weight.shape
    features = gather_features(local_rows)
    values = weight.astype(jnp.float32)
    quant = soft_clip(values, clip_upper, clip_lower).astype(jnp.bfloat16)
    features, quant = lax.optimization_barrier((features, quant))
    pieces = features.reshape(length, shards, rows).transpose(1, 0, 2)
    mine = lax.all_to_all(pieces, "fsdp", 0, 0)
    inputs = mine.reshape(shards * length, rows)

    partial = jnp.dot(inputs, quant, preferred_element_type=jnp.float32).reshape(shards, length, columns)
    me = lax.axis_index("fsdp")
    received = lax.all_to_all(partial.astype(jnp.float16), "fsdp", 0, 0).astype(jnp.float32)
    others = jnp.where((jnp.arange(shards) == me)[:, None, None], 0.0, received)
    own = lax.dynamic_index_in_dim(partial, me, 0, keepdims=False)
    proj = (own + jnp.sum(others, axis=0)).astype(jnp.bfloat16)

    taps = jnp.repeat(filters, CGROUP, axis=0).T
    pad = FILT - 1
    previous = from_behind(proj[length - pad :], "ctx", 1)
    padded = jnp.concatenate([previous, proj], axis=0).astype(jnp.float32)
    conv = jnp.zeros((length, columns), jnp.float32)
    for tap in range(FILT):
        conv = conv + taps[tap] * padded[pad - tap : pad - tap + length]
    gates = gate.reshape(length, columns).astype(jnp.float32)
    wanted = target.reshape(length, columns).astype(jnp.float32)
    total_tokens = lax.axis_size("fsdp") * lax.axis_size("ctx") * length
    scale = 1024.0 / jnp.sqrt(jnp.float32(total_tokens))
    d_conv = scale * (gates * conv - wanted) * gates
    following = from_behind(d_conv[:pad], "ctx", -1)
    padded_back = jnp.concatenate([d_conv, following], axis=0)
    d_proj = jnp.zeros((length, columns), jnp.float32)
    for tap in range(FILT):
        d_proj = d_proj + taps[tap] * padded_back[tap : tap + length]
    d_proj = d_proj.astype(jnp.bfloat16)

    copies = jnp.broadcast_to(d_proj[None], (shards, length, columns))
    d_all = lax.all_to_all(copies, "fsdp", 0, 0).reshape(shards * length, columns)
    d_clipped = lax.dot_general(
        inputs, d_all, (((0,), (0,)), ((), ())), preferred_element_type=jnp.float32
    )
    _, pull = jax.vjp(
        lambda upper_logit, lower_logit: soft_clip(values, upper_logit, lower_logit),
        clip_upper,
        clip_lower,
    )
    grad_up, grad_low = pull(d_clipped)
    grad_upper, grad_lower = sum_over_ctx(grad_up), sum_over_ctx(grad_low)
    return (grad_upper, grad_lower)


def solution(mesh):
    return jax.shard_map(
        on_device,
        mesh=mesh,
        in_specs=(
            P(("parts", "fsdp"), "ctx", None, "seq"),
            P("fsdp", "seq"),
            P(("parts", "fsdp"), "seq"),
            P(("parts", "fsdp"), "seq"),
            P("seq", None),
            P(("parts", "fsdp"), "ctx", None, "seq"),
            P(("parts", "fsdp"), "ctx", None, "seq"),
        ),
        out_specs=(P(("parts", "fsdp"), "seq"), P(("parts", "fsdp"), "seq")),
        check_vma=False,
    )
```

```python
import jax
import jax.numpy as jnp
from jax import lax
from jax.sharding import PartitionSpec as P

FILT = 7
CGROUP = 16


def from_behind(value, axis, by):
    devices = lax.axis_size(axis)
    pairs = [(i, i + by) for i in range(devices) if 0 <= i + by < devices]
    return lax.ppermute(value, axis, pairs)


def soft_clip(values, upper_logit, lower_logit):
    rows = values.shape[0]
    groups = upper_logit.shape[0]
    blocks = values.reshape(groups, rows // groups, values.shape[1])
    amax = jnp.max(jnp.abs(blocks), axis=1) + 1e-06
    upper = jax.nn.sigmoid(upper_logit) * amax
    lower = -jax.nn.sigmoid(lower_logit) * amax
    center = ((upper + lower) * 0.5)[:, None, :]
    radius = ((upper - lower) * 0.5)[:, None, :]
    clipped = center + radius * jnp.tanh((blocks - center) / radius)
    return clipped.reshape(rows, values.shape[1])


def gather_features(local_rows):
    devices = lax.axis_size("seq")
    if devices != 2:
        return lax.all_gather(local_rows, "seq", axis=1, tiled=True)
    other = lax.ppermute(local_rows, "seq", [(0, 1), (1, 0)])
    first = lax.axis_index("seq") == 0
    return jnp.where(
        first,
        jnp.concatenate([local_rows, other], axis=1),
        jnp.concatenate([other, local_rows], axis=1),
    )


def sum_over_ctx(value):
    devices = lax.axis_size("ctx")
    if devices != 2:
        return lax.psum(value, "ctx")
    return value + lax.ppermute(value, "ctx", [(0, 1), (1, 0)])


def column_stream(inputs, quant, values, clip_upper, clip_lower, taps, gates, wanted, scale, me, shards, length):
    columns = quant.shape[1]
    partial = jnp.dot(inputs, quant, preferred_element_type=jnp.float32).reshape(shards, length, columns)
    received = lax.all_to_all(partial.astype(jnp.float16), "fsdp", 0, 0).astype(jnp.float32)
    others = jnp.where((jnp.arange(shards) == me)[:, None, None], 0.0, received)
    own = lax.dynamic_index_in_dim(partial, me, 0, keepdims=False)
    proj = (own + jnp.sum(others, axis=0)).astype(jnp.bfloat16)

    pad = FILT - 1
    previous = from_behind(proj[length - pad :], "ctx", 1)
    padded = jnp.concatenate([previous, proj], axis=0).astype(jnp.float32)
    conv = jnp.zeros((length, columns), jnp.float32)
    for tap in range(FILT):
        conv = conv + taps[tap] * padded[pad - tap : pad - tap + length]
    gates = gates.astype(jnp.float32)
    wanted = wanted.astype(jnp.float32)
    d_conv = scale * (gates * conv - wanted) * gates
    following = from_behind(d_conv[:pad], "ctx", -1)
    padded_back = jnp.concatenate([d_conv, following], axis=0)
    d_proj = jnp.zeros((length, columns), jnp.float32)
    for tap in range(FILT):
        d_proj = d_proj + taps[tap] * padded_back[tap : tap + length]
    d_proj = d_proj.astype(jnp.bfloat16)

    copies = jnp.broadcast_to(d_proj[None], (shards, length, columns))
    d_all = lax.all_to_all(copies, "fsdp", 0, 0).reshape(shards * length, columns)
    d_clipped = lax.dot_general(
        inputs, d_all, (((0,), (0,)), ((), ())), preferred_element_type=jnp.float32
    )
    _, pull = jax.vjp(
        lambda upper_logit, lower_logit: soft_clip(values, upper_logit, lower_logit),
        clip_upper,
        clip_lower,
    )
    return pull(d_clipped)


def on_device(hidden_in, weight, clip_upper, clip_lower, filters, gate, target):
    shards = lax.axis_size("fsdp")
    width = hidden_in.shape[-1]
    local_rows = hidden_in.reshape(-1, width)
    length = local_rows.shape[0]
    rows, columns = weight.shape
    features = gather_features(local_rows)
    values = weight.astype(jnp.float32)
    quant = soft_clip(values, clip_upper, clip_lower).astype(jnp.bfloat16)
    features, quant = lax.optimization_barrier((features, quant))
    pieces = features.reshape(length, shards, rows).transpose(1, 0, 2)
    mine = lax.all_to_all(pieces, "fsdp", 0, 0)
    inputs = mine.reshape(shards * length, rows)

    taps_all = jnp.repeat(filters, CGROUP, axis=0).T
    gates_all = gate.reshape(length, columns)
    wanted_all = target.reshape(length, columns)
    total_tokens = lax.axis_size("fsdp") * lax.axis_size("ctx") * length
    scale = 1024.0 / jnp.sqrt(jnp.float32(total_tokens))
    me = lax.axis_index("fsdp")
    streams = 2 if columns % (2 * 128) == 0 else 1
    width_of = columns // streams
    ups, lows = [], []
    for stream in range(streams):
        cols = slice(stream * width_of, (stream + 1) * width_of)
        grad_up, grad_low = column_stream(
            inputs, quant[:, cols], values[:, cols], clip_upper[:, cols], clip_lower[:, cols],
            taps_all[:, cols], gates_all[:, cols], wanted_all[:, cols], scale, me, shards, length,
        )
        ups.append(grad_up)
        lows.append(grad_low)
    grad_up = jnp.concatenate(ups, axis=1)
    grad_low = jnp.concatenate(lows, axis=1)
    grad_upper, grad_lower = sum_over_ctx(grad_up), sum_over_ctx(grad_low)
    return (grad_upper, grad_lower)


def solution(mesh):
    return jax.shard_map(
        on_device,
        mesh=mesh,
        in_specs=(
            P(("parts", "fsdp"), "ctx", None, "seq"),
            P("fsdp", "seq"),
            P(("parts", "fsdp"), "seq"),
            P(("parts", "fsdp"), "seq"),
            P("seq", None),
            P(("parts", "fsdp"), "ctx", None, "seq"),
            P(("parts", "fsdp"), "ctx", None, "seq"),
        ),
        out_specs=(P(("parts", "fsdp"), "seq"), P(("parts", "fsdp"), "seq")),
        check_vma=False,
    )
```

```python
import jax
import jax.numpy as jnp
from jax import lax
from jax.sharding import PartitionSpec as P

FILT = 7
CGROUP = 16


def from_behind(value, axis, by):
    devices = lax.axis_size(axis)
    pairs = [(i, i + by) for i in range(devices) if 0 <= i + by < devices]
    return lax.ppermute(value, axis, pairs)


def soft_clip(values, upper_logit, lower_logit):
    rows = values.shape[0]
    groups = upper_logit.shape[0]
    blocks = values.reshape(groups, rows // groups, values.shape[1])
    amax = jnp.max(jnp.abs(blocks), axis=1) + 1e-06
    upper = jax.nn.sigmoid(upper_logit) * amax
    lower = -jax.nn.sigmoid(lower_logit) * amax
    center = ((upper + lower) * 0.5)[:, None, :]
    radius = ((upper - lower) * 0.5)[:, None, :]
    clipped = center + radius * jnp.tanh((blocks - center) / radius)
    return clipped.reshape(rows, values.shape[1])


def clip_factors(values, upper_logit, lower_logit):
    rows, columns = values.shape
    groups = upper_logit.shape[0]
    blocks = values.reshape(groups, rows // groups, columns)
    amax = jnp.max(jnp.abs(blocks), axis=1) + 1e-06
    up = jax.nn.sigmoid(upper_logit)
    low = jax.nn.sigmoid(lower_logit)
    upper = up * amax
    lower = -low * amax
    center = ((upper + lower) * 0.5)[:, None, :]
    radius = ((upper - lower) * 0.5)[:, None, :]
    z = (blocks - center) / radius
    t = jnp.tanh(z)
    square = t * t
    slope = t - (1.0 - square) * z
    toward_upper = (square + slope).reshape(rows, columns)
    toward_lower = (square - slope).reshape(rows, columns)
    scale_upper = 0.5 * up * (1.0 - up) * amax
    scale_lower = -0.5 * low * (1.0 - low) * amax
    return toward_upper, toward_lower, scale_upper, scale_lower


def gather_features(local_rows):
    devices = lax.axis_size("seq")
    if devices != 2:
        return lax.all_gather(local_rows, "seq", axis=1, tiled=True)
    other = lax.ppermute(local_rows, "seq", [(0, 1), (1, 0)])
    first = lax.axis_index("seq") == 0
    return jnp.where(
        first,
        jnp.concatenate([local_rows, other], axis=1),
        jnp.concatenate([other, local_rows], axis=1),
    )


def sum_over_ctx(value):
    devices = lax.axis_size("ctx")
    if devices != 2:
        return lax.psum(value, "ctx")
    return value + lax.ppermute(value, "ctx", [(0, 1), (1, 0)])


def column_stream(inputs, quant, factors, taps, gates, wanted, scale, me, shards, length):
    columns = quant.shape[1]
    partial = jnp.dot(inputs, quant, preferred_element_type=jnp.float32).reshape(shards, length, columns)
    received = lax.all_to_all(partial.astype(jnp.float16), "fsdp", 0, 0).astype(jnp.float32)
    others = jnp.where((jnp.arange(shards) == me)[:, None, None], 0.0, received)
    own = lax.dynamic_index_in_dim(partial, me, 0, keepdims=False)
    proj = (own + jnp.sum(others, axis=0)).astype(jnp.bfloat16)

    pad = FILT - 1
    previous = from_behind(proj[length - pad :], "ctx", 1)
    padded = jnp.concatenate([previous, proj], axis=0).astype(jnp.float32)
    conv = jnp.zeros((length, columns), jnp.float32)
    for tap in range(FILT):
        conv = conv + taps[tap] * padded[pad - tap : pad - tap + length]
    gates = gates.astype(jnp.float32)
    wanted = wanted.astype(jnp.float32)
    d_conv = scale * (gates * conv - wanted) * gates
    following = from_behind(d_conv[:pad], "ctx", -1)
    padded_back = jnp.concatenate([d_conv, following], axis=0)
    d_proj = jnp.zeros((length, columns), jnp.float32)
    for tap in range(FILT):
        d_proj = d_proj + taps[tap] * padded_back[tap : tap + length]
    d_proj = d_proj.astype(jnp.bfloat16)

    copies = jnp.broadcast_to(d_proj[None], (shards, length, columns))
    d_all = lax.all_to_all(copies, "fsdp", 0, 0).reshape(shards * length, columns)
    d_clipped = lax.dot_general(
        inputs, d_all, (((0,), (0,)), ((), ())), preferred_element_type=jnp.float32
    )
    toward_upper, toward_lower, scale_upper, scale_lower = factors
    groups = scale_upper.shape[0]
    grouped = d_clipped.reshape(groups, -1, columns)
    grad_up = jnp.sum(grouped * toward_upper.reshape(groups, -1, columns), axis=1) * scale_upper
    grad_low = jnp.sum(grouped * toward_lower.reshape(groups, -1, columns), axis=1) * scale_lower
    return grad_up, grad_low


def on_device(hidden_in, weight, clip_upper, clip_lower, filters, gate, target):
    shards = lax.axis_size("fsdp")
    width = hidden_in.shape[-1]
    local_rows = hidden_in.reshape(-1, width)
    length = local_rows.shape[0]
    rows, columns = weight.shape
    features = gather_features(local_rows)
    values = weight.astype(jnp.float32)
    quant = soft_clip(values, clip_upper, clip_lower).astype(jnp.bfloat16)
    features, quant = lax.optimization_barrier((features, quant))
    pieces = features.reshape(length, shards, rows).transpose(1, 0, 2)
    mine = lax.all_to_all(pieces, "fsdp", 0, 0)
    inputs = mine.reshape(shards * length, rows)

    factors = clip_factors(values, clip_upper, clip_lower)
    taps_all = jnp.repeat(filters, CGROUP, axis=0).T
    gates_all = gate.reshape(length, columns)
    wanted_all = target.reshape(length, columns)
    total_tokens = lax.axis_size("fsdp") * lax.axis_size("ctx") * length
    scale = 1024.0 / jnp.sqrt(jnp.float32(total_tokens))
    me = lax.axis_index("fsdp")
    streams = 2 if columns % (2 * 128) == 0 else 1
    width_of = columns // streams
    ups, lows = [], []
    for stream in range(streams):
        cols = slice(stream * width_of, (stream + 1) * width_of)
        grad_up, grad_low = column_stream(
            inputs, quant[:, cols], [factor[:, cols] for factor in factors],
            taps_all[:, cols], gates_all[:, cols], wanted_all[:, cols], scale, me, shards, length,
        )
        ups.append(grad_up)
        lows.append(grad_low)
    grad_up = jnp.concatenate(ups, axis=1)
    grad_low = jnp.concatenate(lows, axis=1)
    grad_upper, grad_lower = sum_over_ctx(grad_up), sum_over_ctx(grad_low)
    return (grad_upper, grad_lower)


def solution(mesh):
    return jax.shard_map(
        on_device,
        mesh=mesh,
        in_specs=(
            P(("parts", "fsdp"), "ctx", None, "seq"),
            P("fsdp", "seq"),
            P(("parts", "fsdp"), "seq"),
            P(("parts", "fsdp"), "seq"),
            P("seq", None),
            P(("parts", "fsdp"), "ctx", None, "seq"),
            P(("parts", "fsdp"), "ctx", None, "seq"),
        ),
        out_specs=(P(("parts", "fsdp"), "seq"), P(("parts", "fsdp"), "seq")),
        check_vma=False,
    )
```

```python
import jax
import jax.numpy as jnp
from jax import lax
from jax.sharding import PartitionSpec as P

FILT = 7
CGROUP = 16


def from_behind(value, axis, by):
    devices = lax.axis_size(axis)
    pairs = [(i, i + by) for i in range(devices) if 0 <= i + by < devices]
    return lax.ppermute(value, axis, pairs)


def soft_clip(values, upper_logit, lower_logit):
    rows = values.shape[0]
    groups = upper_logit.shape[0]
    blocks = values.reshape(groups, rows // groups, values.shape[1])
    amax = jnp.max(jnp.abs(blocks), axis=1) + 1e-06
    upper = jax.nn.sigmoid(upper_logit) * amax
    lower = -jax.nn.sigmoid(lower_logit) * amax
    center = ((upper + lower) * 0.5)[:, None, :]
    radius = ((upper - lower) * 0.5)[:, None, :]
    clipped = center + radius * jnp.tanh((blocks - center) / radius)
    return clipped.reshape(rows, values.shape[1])


def gather_features(local_rows):
    devices = lax.axis_size("seq")
    if devices != 2:
        return lax.all_gather(local_rows, "seq", axis=1, tiled=True)
    other = lax.ppermute(local_rows, "seq", [(0, 1), (1, 0)])
    first = lax.axis_index("seq") == 0
    return jnp.where(
        first,
        jnp.concatenate([local_rows, other], axis=1),
        jnp.concatenate([other, local_rows], axis=1),
    )


def rows_of_block(local_rows, shards, rows):
    devices = lax.axis_size("seq")
    length = local_rows.shape[0]
    if devices != 2 or length % 2:
        features = gather_features(local_rows)
        pieces = features.reshape(length, shards, rows).transpose(1, 0, 2)
        return lax.all_to_all(pieces, "fsdp", 0, 0)
    half = length // 2
    first = lax.axis_index("seq") == 0
    wanted_by_other = lax.dynamic_slice_in_dim(local_rows, jnp.where(first, half, 0), half, 0)
    kept = lax.dynamic_slice_in_dim(local_rows, jnp.where(first, 0, half), half, 0)
    other = lax.ppermute(wanted_by_other, "seq", [(0, 1), (1, 0)])
    features = jnp.where(
        first, jnp.concatenate([kept, other], axis=1), jnp.concatenate([other, kept], axis=1)
    )
    pieces = features.reshape(half, shards, rows).transpose(1, 0, 2)
    own_half = lax.all_to_all(pieces, "fsdp", 0, 0)
    other_half = lax.ppermute(own_half, "seq", [(0, 1), (1, 0)])
    return jnp.where(
        first,
        jnp.concatenate([own_half, other_half], axis=1),
        jnp.concatenate([other_half, own_half], axis=1),
    )


def sum_over_ctx(value):
    devices = lax.axis_size("ctx")
    if devices != 2:
        return lax.psum(value, "ctx")
    return value + lax.ppermute(value, "ctx", [(0, 1), (1, 0)])


def on_device(hidden_in, weight, clip_upper, clip_lower, filters, gate, target):
    shards = lax.axis_size("fsdp")
    width = hidden_in.shape[-1]
    local_rows = hidden_in.reshape(-1, width)
    length = local_rows.shape[0]
    rows, columns = weight.shape
    values = weight.astype(jnp.float32)
    quant = soft_clip(values, clip_upper, clip_lower).astype(jnp.bfloat16)
    mine = rows_of_block(local_rows, shards, rows)
    mine, quant = lax.optimization_barrier((mine, quant))
    inputs = mine.reshape(shards * length, rows)

    partial = jnp.dot(inputs, quant, preferred_element_type=jnp.float32).reshape(shards, length, columns)
    me = lax.axis_index("fsdp")
    received = lax.all_to_all(partial.astype(jnp.float16), "fsdp", 0, 0).astype(jnp.float32)
    others = jnp.where((jnp.arange(shards) == me)[:, None, None], 0.0, received)
    own = lax.dynamic_index_in_dim(partial, me, 0, keepdims=False)
    proj = (own + jnp.sum(others, axis=0)).astype(jnp.bfloat16)

    taps = jnp.repeat(filters, CGROUP, axis=0).T
    pad = FILT - 1
    previous = from_behind(proj[length - pad :], "ctx", 1)
    padded = jnp.concatenate([previous, proj], axis=0).astype(jnp.float32)
    conv = jnp.zeros((length, columns), jnp.float32)
    for tap in range(FILT):
        conv = conv + taps[tap] * padded[pad - tap : pad - tap + length]
    gates = gate.reshape(length, columns).astype(jnp.float32)
    wanted = target.reshape(length, columns).astype(jnp.float32)
    total_tokens = lax.axis_size("fsdp") * lax.axis_size("ctx") * length
    scale = 1024.0 / jnp.sqrt(jnp.float32(total_tokens))
    d_conv = scale * (gates * conv - wanted) * gates
    following = from_behind(d_conv[:pad], "ctx", -1)
    padded_back = jnp.concatenate([d_conv, following], axis=0)
    d_proj = jnp.zeros((length, columns), jnp.float32)
    for tap in range(FILT):
        d_proj = d_proj + taps[tap] * padded_back[tap : tap + length]
    d_proj = d_proj.astype(jnp.bfloat16)

    copies = jnp.broadcast_to(d_proj[None], (shards, length, columns))
    d_all = lax.all_to_all(copies, "fsdp", 0, 0).reshape(shards * length, columns)
    d_clipped = lax.dot_general(
        inputs, d_all, (((0,), (0,)), ((), ())), preferred_element_type=jnp.float32
    )
    _, pull = jax.vjp(
        lambda upper_logit, lower_logit: soft_clip(values, upper_logit, lower_logit),
        clip_upper,
        clip_lower,
    )
    grad_up, grad_low = pull(d_clipped)
    grad_upper, grad_lower = sum_over_ctx(grad_up), sum_over_ctx(grad_low)
    return (grad_upper, grad_lower)


def solution(mesh):
    return jax.shard_map(
        on_device,
        mesh=mesh,
        in_specs=(
            P(("parts", "fsdp"), "ctx", None, "seq"),
            P("fsdp", "seq"),
            P(("parts", "fsdp"), "seq"),
            P(("parts", "fsdp"), "seq"),
            P("seq", None),
            P(("parts", "fsdp"), "ctx", None, "seq"),
            P(("parts", "fsdp"), "ctx", None, "seq"),
        ),
        out_specs=(P(("parts", "fsdp"), "seq"), P(("parts", "fsdp"), "seq")),
        check_vma=False,
    )
```

```python
import jax
import jax.numpy as jnp
from jax import lax
from jax.sharding import PartitionSpec as P

FILT = 7
CGROUP = 16


def from_behind(value, axis, by):
    devices = lax.axis_size(axis)
    pairs = [(i, i + by) for i in range(devices) if 0 <= i + by < devices]
    return lax.ppermute(value, axis, pairs)


def clip_bounds(values, upper_logit, lower_logit):
    rows = values.shape[0]
    groups = upper_logit.shape[0]
    blocks = values.reshape(groups, rows // groups, values.shape[1])
    amax = jnp.max(jnp.abs(blocks), axis=1) + 1e-06
    upper = jax.nn.sigmoid(upper_logit) * amax
    lower = -jax.nn.sigmoid(lower_logit) * amax
    center = ((upper + lower) * 0.5)[:, None, :]
    radius = ((upper - lower) * 0.5)[:, None, :]
    return blocks, amax, center, radius


def soft_clip(values, upper_logit, lower_logit):
    blocks, _, center, radius = clip_bounds(values, upper_logit, lower_logit)
    clipped = center + radius * jnp.tanh((blocks - center) * (1.0 / radius))
    return clipped.reshape(values.shape)


def soft_clip_grads(values, upper_logit, lower_logit, d_clipped):
    blocks, amax, center, radius = clip_bounds(values, upper_logit, lower_logit)
    z = (blocks - center) * (1.0 / radius)
    t = jnp.tanh(z)
    square = t * t
    slope = t - (1.0 - square) * z
    grouped = d_clipped.reshape(blocks.shape)
    toward_upper = jnp.sum(grouped * (square + slope), axis=1)
    toward_lower = jnp.sum(grouped * (square - slope), axis=1)
    up = jax.nn.sigmoid(upper_logit)
    low = jax.nn.sigmoid(lower_logit)
    grad_up = toward_upper * (0.5 * up * (1.0 - up) * amax)
    grad_low = toward_lower * (-0.5 * low * (1.0 - low) * amax)
    return grad_up, grad_low


def gather_features(local_rows):
    devices = lax.axis_size("seq")
    if devices != 2:
        return lax.all_gather(local_rows, "seq", axis=1, tiled=True)
    other = lax.ppermute(local_rows, "seq", [(0, 1), (1, 0)])
    first = lax.axis_index("seq") == 0
    return jnp.where(
        first,
        jnp.concatenate([local_rows, other], axis=1),
        jnp.concatenate([other, local_rows], axis=1),
    )


def rows_of_block(local_rows, shards, rows):
    devices = lax.axis_size("seq")
    length = local_rows.shape[0]
    if devices != 2 or length % 2:
        features = gather_features(local_rows)
        pieces = features.reshape(length, shards, rows).transpose(1, 0, 2)
        return lax.all_to_all(pieces, "fsdp", 0, 0)
    half = length // 2
    first = lax.axis_index("seq") == 0
    wanted_by_other = lax.dynamic_slice_in_dim(local_rows, jnp.where(first, half, 0), half, 0)
    kept = lax.dynamic_slice_in_dim(local_rows, jnp.where(first, 0, half), half, 0)
    other = lax.ppermute(wanted_by_other, "seq", [(0, 1), (1, 0)])
    features = jnp.where(
        first, jnp.concatenate([kept, other], axis=1), jnp.concatenate([other, kept], axis=1)
    )
    pieces = features.reshape(half, shards, rows).transpose(1, 0, 2)
    own_half = lax.all_to_all(pieces, "fsdp", 0, 0)
    other_half = lax.ppermute(own_half, "seq", [(0, 1), (1, 0)])
    return jnp.where(
        first,
        jnp.concatenate([own_half, other_half], axis=1),
        jnp.concatenate([other_half, own_half], axis=1),
    )


def sum_over_ctx(value):
    devices = lax.axis_size("ctx")
    if devices != 2:
        return lax.psum(value, "ctx")
    return value + lax.ppermute(value, "ctx", [(0, 1), (1, 0)])


def on_device(hidden_in, weight, clip_upper, clip_lower, filters, gate, target):
    shards = lax.axis_size("fsdp")
    width = hidden_in.shape[-1]
    local_rows = hidden_in.reshape(-1, width)
    length = local_rows.shape[0]
    rows, columns = weight.shape
    values = weight.astype(jnp.float32)
    quant = soft_clip(values, clip_upper, clip_lower).astype(jnp.bfloat16)
    mine = rows_of_block(local_rows, shards, rows)
    mine, quant = lax.optimization_barrier((mine, quant))
    inputs = mine.reshape(shards * length, rows)

    partial = jnp.dot(inputs, quant, preferred_element_type=jnp.float32).reshape(shards, length, columns)
    me = lax.axis_index("fsdp")
    received = lax.all_to_all(partial.astype(jnp.float16), "fsdp", 0, 0).astype(jnp.float32)
    others = jnp.where((jnp.arange(shards) == me)[:, None, None], 0.0, received)
    own = lax.dynamic_index_in_dim(partial, me, 0, keepdims=False)
    proj = (own + jnp.sum(others, axis=0)).astype(jnp.bfloat16)

    taps = jnp.repeat(filters, CGROUP, axis=0).T
    pad = FILT - 1
    previous = from_behind(proj[length - pad :], "ctx", 1)
    padded = jnp.concatenate([previous, proj], axis=0).astype(jnp.float32)
    conv = jnp.zeros((length, columns), jnp.float32)
    for tap in range(FILT):
        conv = conv + taps[tap] * padded[pad - tap : pad - tap + length]
    gates = gate.reshape(length, columns).astype(jnp.float32)
    wanted = target.reshape(length, columns).astype(jnp.float32)
    total_tokens = lax.axis_size("fsdp") * lax.axis_size("ctx") * length
    scale = 1024.0 / jnp.sqrt(jnp.float32(total_tokens))
    d_conv = scale * (gates * conv - wanted) * gates
    following = from_behind(d_conv[:pad], "ctx", -1)
    padded_back = jnp.concatenate([d_conv, following], axis=0)
    d_proj = jnp.zeros((length, columns), jnp.float32)
    for tap in range(FILT):
        d_proj = d_proj + taps[tap] * padded_back[tap : tap + length]
    d_proj = d_proj.astype(jnp.bfloat16)

    copies = jnp.broadcast_to(d_proj[None], (shards, length, columns))
    d_all = lax.all_to_all(copies, "fsdp", 0, 0).reshape(shards * length, columns)
    d_clipped = lax.dot_general(
        inputs, d_all, (((0,), (0,)), ((), ())), preferred_element_type=jnp.float32
    )
    grad_up, grad_low = soft_clip_grads(values, clip_upper, clip_lower, d_clipped)
    grad_upper, grad_lower = sum_over_ctx(grad_up), sum_over_ctx(grad_low)
    return (grad_upper, grad_lower)


def solution(mesh):
    return jax.shard_map(
        on_device,
        mesh=mesh,
        in_specs=(
            P(("parts", "fsdp"), "ctx", None, "seq"),
            P("fsdp", "seq"),
            P(("parts", "fsdp"), "seq"),
            P(("parts", "fsdp"), "seq"),
            P("seq", None),
            P(("parts", "fsdp"), "ctx", None, "seq"),
            P(("parts", "fsdp"), "ctx", None, "seq"),
        ),
        out_specs=(P(("parts", "fsdp"), "seq"), P(("parts", "fsdp"), "seq")),
        check_vma=False,
    )
```

```python
import jax
import jax.numpy as jnp
from jax import lax
from jax.sharding import PartitionSpec as P

FILT = 7
CGROUP = 16


def from_behind(value, axis, by):
    devices = lax.axis_size(axis)
    pairs = [(i, i + by) for i in range(devices) if 0 <= i + by < devices]
    return lax.ppermute(value, axis, pairs)


def clip_bounds(values, upper_logit, lower_logit):
    rows = values.shape[0]
    groups = upper_logit.shape[0]
    blocks = values.reshape(groups, rows // groups, values.shape[1])
    amax = jnp.max(jnp.abs(blocks), axis=1) + 1e-06
    upper = jax.nn.sigmoid(upper_logit) * amax
    lower = -jax.nn.sigmoid(lower_logit) * amax
    center = ((upper + lower) * 0.5)[:, None, :]
    radius = ((upper - lower) * 0.5)[:, None, :]
    return blocks, amax, center, radius


def soft_clip(values, upper_logit, lower_logit):
    blocks, _, center, radius = clip_bounds(values, upper_logit, lower_logit)
    clipped = center + radius * jnp.tanh((blocks - center) * (1.0 / radius))
    return clipped.reshape(values.shape)


def soft_clip_grads(values, upper_logit, lower_logit, d_clipped):
    blocks, amax, center, radius = clip_bounds(values, upper_logit, lower_logit)
    z = (blocks - center) * (1.0 / radius)
    t = jnp.tanh(z)
    square = t * t
    slope = t - (1.0 - square) * z
    grouped = d_clipped.reshape(blocks.shape)
    toward_upper = jnp.sum(grouped * (square + slope), axis=1)
    toward_lower = jnp.sum(grouped * (square - slope), axis=1)
    up = jax.nn.sigmoid(upper_logit)
    low = jax.nn.sigmoid(lower_logit)
    grad_up = toward_upper * (0.5 * up * (1.0 - up) * amax)
    grad_low = toward_lower * (-0.5 * low * (1.0 - low) * amax)
    return grad_up, grad_low


def gather_features(local_rows):
    devices = lax.axis_size("seq")
    if devices != 2:
        return lax.all_gather(local_rows, "seq", axis=1, tiled=True)
    other = lax.ppermute(local_rows, "seq", [(0, 1), (1, 0)])
    first = lax.axis_index("seq") == 0
    return jnp.where(
        first,
        jnp.concatenate([local_rows, other], axis=1),
        jnp.concatenate([other, local_rows], axis=1),
    )


def rows_of_block(local_rows, shards, rows, quant):
    devices = lax.axis_size("seq")
    length = local_rows.shape[0]
    if devices != 2 or length % 2:
        features, quant = lax.optimization_barrier((gather_features(local_rows), quant))
        pieces = features.reshape(length, shards, rows).transpose(1, 0, 2)
        return [(lax.all_to_all(pieces, "fsdp", 0, 0), 0)], quant
    half = length // 2
    first = lax.axis_index("seq") == 0
    wanted_by_other = lax.dynamic_slice_in_dim(local_rows, jnp.where(first, half, 0), half, 0)
    kept = lax.dynamic_slice_in_dim(local_rows, jnp.where(first, 0, half), half, 0)
    other = lax.ppermute(wanted_by_other, "seq", [(0, 1), (1, 0)])
    other, quant = lax.optimization_barrier((other, quant))
    features = jnp.where(
        first, jnp.concatenate([kept, other], axis=1), jnp.concatenate([other, kept], axis=1)
    )
    pieces = features.reshape(half, shards, rows).transpose(1, 0, 2)
    own_half = lax.all_to_all(pieces, "fsdp", 0, 0)
    other_half = lax.ppermute(own_half, "seq", [(0, 1), (1, 0)])
    own_at = jnp.where(first, 0, half)
    return [(own_half, own_at), (other_half, half - own_at)], quant


def reduce_partial(partial, me):
    shards = partial.shape[0]
    received = lax.all_to_all(partial.astype(jnp.float16), "fsdp", 0, 0).astype(jnp.float32)
    others = jnp.where((jnp.arange(shards) == me)[:, None, None], 0.0, received)
    own = lax.dynamic_index_in_dim(partial, me, 0, keepdims=False)
    return own + jnp.sum(others, axis=0)


def sum_over_ctx(value):
    devices = lax.axis_size("ctx")
    if devices != 2:
        return lax.psum(value, "ctx")
    return value + lax.ppermute(value, "ctx", [(0, 1), (1, 0)])


def on_device(hidden_in, weight, clip_upper, clip_lower, filters, gate, target):
    shards = lax.axis_size("fsdp")
    width = hidden_in.shape[-1]
    local_rows = hidden_in.reshape(-1, width)
    length = local_rows.shape[0]
    rows, columns = weight.shape
    values = weight.astype(jnp.float32)
    quant = soft_clip(values, clip_upper, clip_lower).astype(jnp.bfloat16)
    pieces, quant = rows_of_block(local_rows, shards, rows, quant)
    me = lax.axis_index("fsdp")
    proj = jnp.zeros((length, columns), jnp.float32)
    mine = jnp.zeros((shards, length, rows), local_rows.dtype)
    for piece, at in pieces:
        count = piece.shape[1]
        flat = piece.reshape(shards * count, rows)
        partial = jnp.dot(flat, quant, preferred_element_type=jnp.float32).reshape(shards, count, columns)
        proj = lax.dynamic_update_slice_in_dim(proj, reduce_partial(partial, me), at, 0)
        mine = lax.dynamic_update_slice_in_dim(mine, piece, at, 1)
    proj = proj.astype(jnp.bfloat16)
    inputs = mine.reshape(shards * length, rows)

    taps = jnp.repeat(filters, CGROUP, axis=0).T
    pad = FILT - 1
    previous = from_behind(proj[length - pad :], "ctx", 1)
    padded = jnp.concatenate([previous, proj], axis=0).astype(jnp.float32)
    conv = jnp.zeros((length, columns), jnp.float32)
    for tap in range(FILT):
        conv = conv + taps[tap] * padded[pad - tap : pad - tap + length]
    gates = gate.reshape(length, columns).astype(jnp.float32)
    wanted = target.reshape(length, columns).astype(jnp.float32)
    total_tokens = lax.axis_size("fsdp") * lax.axis_size("ctx") * length
    scale = 1024.0 / jnp.sqrt(jnp.float32(total_tokens))
    d_conv = scale * (gates * conv - wanted) * gates
    following = from_behind(d_conv[:pad], "ctx", -1)
    padded_back = jnp.concatenate([d_conv, following], axis=0)
    d_proj = jnp.zeros((length, columns), jnp.float32)
    for tap in range(FILT):
        d_proj = d_proj + taps[tap] * padded_back[tap : tap + length]
    d_proj = d_proj.astype(jnp.bfloat16)

    copies = jnp.broadcast_to(d_proj[None], (shards, length, columns))
    d_all = lax.all_to_all(copies, "fsdp", 0, 0).reshape(shards * length, columns)
    d_clipped = lax.dot_general(
        inputs, d_all, (((0,), (0,)), ((), ())), preferred_element_type=jnp.float32
    )
    grad_up, grad_low = soft_clip_grads(values, clip_upper, clip_lower, d_clipped)
    grad_upper, grad_lower = sum_over_ctx(grad_up), sum_over_ctx(grad_low)
    return (grad_upper, grad_lower)


def solution(mesh):
    return jax.shard_map(
        on_device,
        mesh=mesh,
        in_specs=(
            P(("parts", "fsdp"), "ctx", None, "seq"),
            P("fsdp", "seq"),
            P(("parts", "fsdp"), "seq"),
            P(("parts", "fsdp"), "seq"),
            P("seq", None),
            P(("parts", "fsdp"), "ctx", None, "seq"),
            P(("parts", "fsdp"), "ctx", None, "seq"),
        ),
        out_specs=(P(("parts", "fsdp"), "seq"), P(("parts", "fsdp"), "seq")),
        check_vma=False,
    )
```

```python
import jax
import jax.numpy as jnp
from jax import lax
from jax.sharding import PartitionSpec as P

FILT = 7
CGROUP = 16


def from_behind(value, axis, by):
    devices = lax.axis_size(axis)
    pairs = [(i, i + by) for i in range(devices) if 0 <= i + by < devices]
    return lax.ppermute(value, axis, pairs)


def clip_bounds(values, upper_logit, lower_logit):
    rows = values.shape[0]
    groups = upper_logit.shape[0]
    blocks = values.reshape(groups, rows // groups, values.shape[1])
    amax = jnp.max(jnp.abs(blocks.astype(jnp.bfloat16)), axis=1).astype(jnp.float32) + 1e-06
    upper = jax.nn.sigmoid(upper_logit) * amax
    lower = -jax.nn.sigmoid(lower_logit) * amax
    center = ((upper + lower) * 0.5)[:, None, :]
    radius = ((upper - lower) * 0.5)[:, None, :]
    return blocks, amax, center, radius


def soft_clip(values, upper_logit, lower_logit):
    blocks, _, center, radius = clip_bounds(values, upper_logit, lower_logit)
    clipped = center + radius * jnp.tanh((blocks - center) * (1.0 / radius))
    return clipped.reshape(values.shape)


def soft_clip_grads(values, upper_logit, lower_logit, d_clipped):
    blocks, amax, center, radius = clip_bounds(values, upper_logit, lower_logit)
    z = (blocks - center) * (1.0 / radius)
    t = jnp.tanh(z)
    square = t * t
    slope = t - (1.0 - square) * z
    grouped = d_clipped.reshape(blocks.shape)
    toward_upper = jnp.sum(grouped * (square + slope), axis=1)
    toward_lower = jnp.sum(grouped * (square - slope), axis=1)
    up = jax.nn.sigmoid(upper_logit)
    low = jax.nn.sigmoid(lower_logit)
    grad_up = toward_upper * (0.5 * up * (1.0 - up) * amax)
    grad_low = toward_lower * (-0.5 * low * (1.0 - low) * amax)
    return grad_up, grad_low


def gather_features(local_rows):
    devices = lax.axis_size("seq")
    if devices != 2:
        return lax.all_gather(local_rows, "seq", axis=1, tiled=True)
    other = lax.ppermute(local_rows, "seq", [(0, 1), (1, 0)])
    first = lax.axis_index("seq") == 0
    return jnp.where(
        first,
        jnp.concatenate([local_rows, other], axis=1),
        jnp.concatenate([other, local_rows], axis=1),
    )


def rows_of_block(local_rows, shards, rows, quant):
    devices = lax.axis_size("seq")
    length = local_rows.shape[0]
    if devices != 2 or length % 2:
        features, quant = lax.optimization_barrier((gather_features(local_rows), quant))
        pieces = features.reshape(length, shards, rows).transpose(1, 0, 2)
        return [(lax.all_to_all(pieces, "fsdp", 0, 0), 0)], quant
    half = length // 2
    first = lax.axis_index("seq") == 0
    wanted_by_other = lax.dynamic_slice_in_dim(local_rows, jnp.where(first, half, 0), half, 0)
    kept = lax.dynamic_slice_in_dim(local_rows, jnp.where(first, 0, half), half, 0)
    other = lax.ppermute(wanted_by_other, "seq", [(0, 1), (1, 0)])
    other, quant = lax.optimization_barrier((other, quant))
    features = jnp.where(
        first, jnp.concatenate([kept, other], axis=1), jnp.concatenate([other, kept], axis=1)
    )
    pieces = features.reshape(half, shards, rows).transpose(1, 0, 2)
    own_half = lax.all_to_all(pieces, "fsdp", 0, 0)
    other_half = lax.ppermute(own_half, "seq", [(0, 1), (1, 0)])
    own_at = jnp.where(first, 0, half)
    return [(own_half, own_at), (other_half, half - own_at)], quant


def reduce_partial(partial, me):
    shards = partial.shape[0]
    received = lax.all_to_all(partial.astype(jnp.float16), "fsdp", 0, 0).astype(jnp.float32)
    others = jnp.where((jnp.arange(shards) == me)[:, None, None], 0.0, received)
    own = lax.dynamic_index_in_dim(partial, me, 0, keepdims=False)
    return own + jnp.sum(others, axis=0)


def sum_over_ctx(value):
    devices = lax.axis_size("ctx")
    if devices != 2:
        return lax.psum(value, "ctx")
    return value + lax.ppermute(value, "ctx", [(0, 1), (1, 0)])


def on_device(hidden_in, weight, clip_upper, clip_lower, filters, gate, target):
    shards = lax.axis_size("fsdp")
    width = hidden_in.shape[-1]
    local_rows = hidden_in.reshape(-1, width)
    length = local_rows.shape[0]
    rows, columns = weight.shape
    values = weight.astype(jnp.float32)
    quant = soft_clip(values, clip_upper, clip_lower).astype(jnp.bfloat16)
    pieces, quant = rows_of_block(local_rows, shards, rows, quant)
    me = lax.axis_index("fsdp")
    proj = jnp.zeros((length, columns), jnp.float32)
    mine = jnp.zeros((shards, length, rows), local_rows.dtype)
    for piece, at in pieces:
        count = piece.shape[1]
        flat = piece.reshape(shards * count, rows)
        partial = jnp.dot(flat, quant, preferred_element_type=jnp.float32).reshape(shards, count, columns)
        proj = lax.dynamic_update_slice_in_dim(proj, reduce_partial(partial, me), at, 0)
        mine = lax.dynamic_update_slice_in_dim(mine, piece, at, 1)
    proj = proj.astype(jnp.bfloat16)
    inputs = mine.reshape(shards * length, rows)

    taps = jnp.repeat(filters, CGROUP, axis=0).T
    pad = FILT - 1
    previous = from_behind(proj[length - pad :], "ctx", 1)
    upcoming = from_behind(proj[:pad], "ctx", -1)
    gates_in = gate.reshape(length, columns)
    wanted_in = target.reshape(length, columns)
    gates_next = from_behind(gates_in[:pad], "ctx", -1)
    wanted_next = from_behind(wanted_in[:pad], "ctx", -1)
    padded = jnp.concatenate([previous, proj, upcoming], axis=0).astype(jnp.float32)
    extent = length + pad
    conv = jnp.zeros((extent, columns), jnp.float32)
    for tap in range(FILT):
        conv = conv + taps[tap] * padded[pad - tap : pad - tap + extent]
    gates = jnp.concatenate([gates_in, gates_next], axis=0).astype(jnp.float32)
    wanted = jnp.concatenate([wanted_in, wanted_next], axis=0).astype(jnp.float32)
    total_tokens = lax.axis_size("fsdp") * lax.axis_size("ctx") * length
    scale = 1024.0 / jnp.sqrt(jnp.float32(total_tokens))
    d_conv = scale * (gates * conv - wanted) * gates
    d_proj = jnp.zeros((length, columns), jnp.float32)
    for tap in range(FILT):
        d_proj = d_proj + taps[tap] * d_conv[tap : tap + length]
    d_proj = d_proj.astype(jnp.bfloat16)

    copies = jnp.broadcast_to(d_proj[None], (shards, length, columns))
    d_all = lax.all_to_all(copies, "fsdp", 0, 0).reshape(shards * length, columns)
    d_clipped = lax.dot_general(
        inputs, d_all, (((0,), (0,)), ((), ())), preferred_element_type=jnp.float32
    )
    grad_up, grad_low = soft_clip_grads(values, clip_upper, clip_lower, d_clipped)
    grad_upper, grad_lower = sum_over_ctx(grad_up), sum_over_ctx(grad_low)
    return (grad_upper, grad_lower)


def solution(mesh):
    return jax.shard_map(
        on_device,
        mesh=mesh,
        in_specs=(
            P(("parts", "fsdp"), "ctx", None, "seq"),
            P("fsdp", "seq"),
            P(("parts", "fsdp"), "seq"),
            P(("parts", "fsdp"), "seq"),
            P("seq", None),
            P(("parts", "fsdp"), "ctx", None, "seq"),
            P(("parts", "fsdp"), "ctx", None, "seq"),
        ),
        out_specs=(P(("parts", "fsdp"), "seq"), P(("parts", "fsdp"), "seq")),
        check_vma=False,
    )
```

```python
import jax
import jax.numpy as jnp
from jax import lax
from jax.sharding import PartitionSpec as P

FILT = 7
CGROUP = 16


def from_behind(value, axis, by):
    devices = lax.axis_size(axis)
    pairs = [(i, i + by) for i in range(devices) if 0 <= i + by < devices]
    return lax.ppermute(value, axis, pairs)


def clip_bounds(values, upper_logit, lower_logit):
    rows = values.shape[0]
    groups = upper_logit.shape[0]
    blocks = values.reshape(groups, rows // groups, values.shape[1])
    amax = jnp.max(jnp.abs(blocks.astype(jnp.bfloat16)), axis=1).astype(jnp.float32) + 1e-06
    upper = jax.nn.sigmoid(upper_logit) * amax
    lower = -jax.nn.sigmoid(lower_logit) * amax
    center = ((upper + lower) * 0.5)[:, None, :]
    radius = ((upper - lower) * 0.5)[:, None, :]
    return blocks, amax, center, radius


def soft_clip(values, upper_logit, lower_logit):
    blocks, _, center, radius = clip_bounds(values, upper_logit, lower_logit)
    return clip_with(blocks, center, radius)


def clip_with(blocks, center, radius):
    clipped = center + radius * jnp.tanh((blocks - center) * (1.0 / radius))
    return clipped.reshape(-1, blocks.shape[2])


def soft_clip_grads(values, upper_logit, lower_logit, d_clipped):
    blocks, amax, center, radius = clip_bounds(values, upper_logit, lower_logit)
    z = (blocks - center) * (1.0 / radius)
    t = jnp.tanh(z)
    square = t * t
    slope = t - (1.0 - square) * z
    grouped = d_clipped.reshape(blocks.shape)
    toward_upper = jnp.sum(grouped * (square + slope), axis=1)
    toward_lower = jnp.sum(grouped * (square - slope), axis=1)
    up = jax.nn.sigmoid(upper_logit)
    low = jax.nn.sigmoid(lower_logit)
    grad_up = toward_upper * (0.5 * up * (1.0 - up) * amax)
    grad_low = toward_lower * (-0.5 * low * (1.0 - low) * amax)
    return grad_up, grad_low


def gather_features(local_rows):
    devices = lax.axis_size("seq")
    if devices != 2:
        return lax.all_gather(local_rows, "seq", axis=1, tiled=True)
    other = lax.ppermute(local_rows, "seq", [(0, 1), (1, 0)])
    first = lax.axis_index("seq") == 0
    return jnp.where(
        first,
        jnp.concatenate([local_rows, other], axis=1),
        jnp.concatenate([other, local_rows], axis=1),
    )


def rows_of_block(local_rows, shards, rows, blocks, bounds):
    devices = lax.axis_size("seq")
    length = local_rows.shape[0]
    if devices != 2 or length % 2:
        features, bounds = lax.optimization_barrier((gather_features(local_rows), bounds))
        quant = clip_with(blocks, *bounds).astype(jnp.bfloat16)
        pieces = features.reshape(length, shards, rows).transpose(1, 0, 2)
        return [(lax.all_to_all(pieces, "fsdp", 0, 0), 0)], quant
    half = length // 2
    first = lax.axis_index("seq") == 0
    wanted_by_other = lax.dynamic_slice_in_dim(local_rows, jnp.where(first, half, 0), half, 0)
    kept = lax.dynamic_slice_in_dim(local_rows, jnp.where(first, 0, half), half, 0)
    other = lax.ppermute(wanted_by_other, "seq", [(0, 1), (1, 0)])
    other, bounds = lax.optimization_barrier((other, bounds))
    quant = clip_with(blocks, *bounds).astype(jnp.bfloat16)
    features = jnp.where(
        first, jnp.concatenate([kept, other], axis=1), jnp.concatenate([other, kept], axis=1)
    )
    pieces = features.reshape(half, shards, rows).transpose(1, 0, 2)
    own_half = lax.all_to_all(pieces, "fsdp", 0, 0)
    own_half, quant = lax.optimization_barrier((own_half, quant))
    other_half = lax.ppermute(own_half, "seq", [(0, 1), (1, 0)])
    own_at = jnp.where(first, 0, half)
    return [(own_half, own_at), (other_half, half - own_at)], quant


def reduce_partial(partial, me):
    shards = partial.shape[0]
    received = lax.all_to_all(partial.astype(jnp.float16), "fsdp", 0, 0).astype(jnp.float32)
    others = jnp.where((jnp.arange(shards) == me)[:, None, None], 0.0, received)
    own = lax.dynamic_index_in_dim(partial, me, 0, keepdims=False)
    return own + jnp.sum(others, axis=0)


def sum_over_ctx(value):
    devices = lax.axis_size("ctx")
    if devices != 2:
        return lax.psum(value, "ctx")
    return value + lax.ppermute(value, "ctx", [(0, 1), (1, 0)])


def on_device(hidden_in, weight, clip_upper, clip_lower, filters, gate, target):
    shards = lax.axis_size("fsdp")
    width = hidden_in.shape[-1]
    local_rows = hidden_in.reshape(-1, width)
    length = local_rows.shape[0]
    rows, columns = weight.shape
    values = weight.astype(jnp.float32)
    blocks, _, center, radius = clip_bounds(values, clip_upper, clip_lower)
    pieces, quant = rows_of_block(local_rows, shards, rows, blocks, (center, radius))
    me = lax.axis_index("fsdp")
    proj = jnp.zeros((length, columns), jnp.float32)
    mine = jnp.zeros((shards, length, rows), local_rows.dtype)
    for piece, at in pieces:
        count = piece.shape[1]
        flat = piece.reshape(shards * count, rows)
        partial = jnp.dot(flat, quant, preferred_element_type=jnp.float32).reshape(shards, count, columns)
        proj = lax.dynamic_update_slice_in_dim(proj, reduce_partial(partial, me), at, 0)
        mine = lax.dynamic_update_slice_in_dim(mine, piece, at, 1)
    proj = proj.astype(jnp.bfloat16)
    inputs = mine.reshape(shards * length, rows)

    taps = jnp.repeat(filters, CGROUP, axis=0).T
    pad = FILT - 1
    previous = from_behind(proj[length - pad :], "ctx", 1)
    upcoming = from_behind(proj[:pad], "ctx", -1)
    gates_in = gate.reshape(length, columns)
    wanted_in = target.reshape(length, columns)
    gates_next = from_behind(gates_in[:pad], "ctx", -1)
    wanted_next = from_behind(wanted_in[:pad], "ctx", -1)
    padded = jnp.concatenate([previous, proj, upcoming], axis=0).astype(jnp.float32)
    extent = length + pad
    conv = jnp.zeros((extent, columns), jnp.float32)
    for tap in range(FILT):
        conv = conv + taps[tap] * padded[pad - tap : pad - tap + extent]
    gates = jnp.concatenate([gates_in, gates_next], axis=0).astype(jnp.float32)
    wanted = jnp.concatenate([wanted_in, wanted_next], axis=0).astype(jnp.float32)
    total_tokens = lax.axis_size("fsdp") * lax.axis_size("ctx") * length
    scale = 1024.0 / jnp.sqrt(jnp.float32(total_tokens))
    d_conv = scale * (gates * conv - wanted) * gates
    d_proj = jnp.zeros((length, columns), jnp.float32)
    for tap in range(FILT):
        d_proj = d_proj + taps[tap] * d_conv[tap : tap + length]
    d_proj = d_proj.astype(jnp.bfloat16)

    copies = jnp.broadcast_to(d_proj[None], (shards, length, columns))
    d_all = lax.all_to_all(copies, "fsdp", 0, 0).reshape(shards * length, columns)
    d_clipped = lax.dot_general(
        inputs, d_all, (((0,), (0,)), ((), ())), preferred_element_type=jnp.float32
    )
    grad_up, grad_low = soft_clip_grads(values, clip_upper, clip_lower, d_clipped)
    grad_upper, grad_lower = sum_over_ctx(grad_up), sum_over_ctx(grad_low)
    return (grad_upper, grad_lower)


def solution(mesh):
    return jax.shard_map(
        on_device,
        mesh=mesh,
        in_specs=(
            P(("parts", "fsdp"), "ctx", None, "seq"),
            P("fsdp", "seq"),
            P(("parts", "fsdp"), "seq"),
            P(("parts", "fsdp"), "seq"),
            P("seq", None),
            P(("parts", "fsdp"), "ctx", None, "seq"),
            P(("parts", "fsdp"), "ctx", None, "seq"),
        ),
        out_specs=(P(("parts", "fsdp"), "seq"), P(("parts", "fsdp"), "seq")),
        check_vma=False,
    )
```

```python
import jax
import jax.numpy as jnp
from jax import lax
from jax.sharding import PartitionSpec as P

FILT = 7
CGROUP = 16


def from_behind(value, axis, by):
    devices = lax.axis_size(axis)
    pairs = [(i, i + by) for i in range(devices) if 0 <= i + by < devices]
    return lax.ppermute(value, axis, pairs)


def clip_bounds(values, upper_logit, lower_logit):
    rows = values.shape[0]
    groups = upper_logit.shape[0]
    blocks = values.reshape(groups, rows // groups, values.shape[1])
    amax = jnp.max(jnp.abs(blocks.astype(jnp.bfloat16)), axis=1).astype(jnp.float32) + 1e-06
    upper = jax.nn.sigmoid(upper_logit) * amax
    lower = -jax.nn.sigmoid(lower_logit) * amax
    center = ((upper + lower) * 0.5)[:, None, :]
    radius = ((upper - lower) * 0.5)[:, None, :]
    return blocks, amax, center, radius


def soft_clip(values, upper_logit, lower_logit):
    blocks, _, center, radius = clip_bounds(values, upper_logit, lower_logit)
    clipped = center + radius * jnp.tanh((blocks - center) * (1.0 / radius))
    return clipped.reshape(values.shape)


def clip_factors(values, upper_logit, lower_logit):
    blocks, amax, center, radius = clip_bounds(values, upper_logit, lower_logit)
    z = (blocks - center) * (1.0 / radius)
    t = jnp.tanh(z)
    square = t * t
    slope = t - (1.0 - square) * z
    up = jax.nn.sigmoid(upper_logit)
    low = jax.nn.sigmoid(lower_logit)
    return square + slope, square - slope, 0.5 * up * (1.0 - up) * amax, -0.5 * low * (1.0 - low) * amax


def soft_clip_grads(factors, d_clipped):
    toward_upper, toward_lower, scale_upper, scale_lower = factors
    grouped = d_clipped.reshape(toward_upper.shape)
    grad_up = jnp.sum(grouped * toward_upper, axis=1) * scale_upper
    grad_low = jnp.sum(grouped * toward_lower, axis=1) * scale_lower
    return grad_up, grad_low


def gather_features(local_rows):
    devices = lax.axis_size("seq")
    if devices != 2:
        return lax.all_gather(local_rows, "seq", axis=1, tiled=True)
    other = lax.ppermute(local_rows, "seq", [(0, 1), (1, 0)])
    first = lax.axis_index("seq") == 0
    return jnp.where(
        first,
        jnp.concatenate([local_rows, other], axis=1),
        jnp.concatenate([other, local_rows], axis=1),
    )


def rows_of_block(local_rows, shards, rows, quant):
    devices = lax.axis_size("seq")
    length = local_rows.shape[0]
    if devices != 2 or length % 2:
        features, quant = lax.optimization_barrier((gather_features(local_rows), quant))
        pieces = features.reshape(length, shards, rows).transpose(1, 0, 2)
        return [(lax.all_to_all(pieces, "fsdp", 0, 0), 0)], quant
    half = length // 2
    first = lax.axis_index("seq") == 0
    wanted_by_other = lax.dynamic_slice_in_dim(local_rows, jnp.where(first, half, 0), half, 0)
    kept = lax.dynamic_slice_in_dim(local_rows, jnp.where(first, 0, half), half, 0)
    other = lax.ppermute(wanted_by_other, "seq", [(0, 1), (1, 0)])
    other, quant = lax.optimization_barrier((other, quant))
    features = jnp.where(
        first, jnp.concatenate([kept, other], axis=1), jnp.concatenate([other, kept], axis=1)
    )
    pieces = features.reshape(half, shards, rows).transpose(1, 0, 2)
    own_half = lax.all_to_all(pieces, "fsdp", 0, 0)
    other_half = lax.ppermute(own_half, "seq", [(0, 1), (1, 0)])
    own_at = jnp.where(first, 0, half)
    return [(own_half, own_at), (other_half, half - own_at)], quant


def reduce_partial(partial, me):
    shards = partial.shape[0]
    received = lax.all_to_all(partial.astype(jnp.float16), "fsdp", 0, 0).astype(jnp.float32)
    others = jnp.where((jnp.arange(shards) == me)[:, None, None], 0.0, received)
    own = lax.dynamic_index_in_dim(partial, me, 0, keepdims=False)
    return own + jnp.sum(others, axis=0)


def sum_over_ctx(value):
    devices = lax.axis_size("ctx")
    if devices != 2:
        return lax.psum(value, "ctx")
    return value + lax.ppermute(value, "ctx", [(0, 1), (1, 0)])


def on_device(hidden_in, weight, clip_upper, clip_lower, filters, gate, target):
    shards = lax.axis_size("fsdp")
    width = hidden_in.shape[-1]
    local_rows = hidden_in.reshape(-1, width)
    length = local_rows.shape[0]
    rows, columns = weight.shape
    values = weight.astype(jnp.float32)
    quant = soft_clip(values, clip_upper, clip_lower).astype(jnp.bfloat16)
    pieces, quant = rows_of_block(local_rows, shards, rows, quant)
    me = lax.axis_index("fsdp")
    proj = jnp.zeros((length, columns), jnp.float32)
    mine = jnp.zeros((shards, length, rows), local_rows.dtype)
    for piece, at in pieces:
        count = piece.shape[1]
        flat = piece.reshape(shards * count, rows)
        partial = jnp.dot(flat, quant, preferred_element_type=jnp.float32).reshape(shards, count, columns)
        proj = lax.dynamic_update_slice_in_dim(proj, reduce_partial(partial, me), at, 0)
        mine = lax.dynamic_update_slice_in_dim(mine, piece, at, 1)
    proj = proj.astype(jnp.bfloat16)
    inputs = mine.reshape(shards * length, rows)

    taps = jnp.repeat(filters, CGROUP, axis=0).T
    pad = FILT - 1
    previous = from_behind(proj[length - pad :], "ctx", 1)
    upcoming = from_behind(proj[:pad], "ctx", -1)
    gates_in = gate.reshape(length, columns)
    wanted_in = target.reshape(length, columns)
    gates_next = from_behind(gates_in[:pad], "ctx", -1)
    wanted_next = from_behind(wanted_in[:pad], "ctx", -1)
    padded = jnp.concatenate([previous, proj, upcoming], axis=0).astype(jnp.float32)
    extent = length + pad
    conv = jnp.zeros((extent, columns), jnp.float32)
    for tap in range(FILT):
        conv = conv + taps[tap] * padded[pad - tap : pad - tap + extent]
    gates = jnp.concatenate([gates_in, gates_next], axis=0).astype(jnp.float32)
    wanted = jnp.concatenate([wanted_in, wanted_next], axis=0).astype(jnp.float32)
    total_tokens = lax.axis_size("fsdp") * lax.axis_size("ctx") * length
    scale = 1024.0 / jnp.sqrt(jnp.float32(total_tokens))
    d_conv = scale * (gates * conv - wanted) * gates
    d_proj = jnp.zeros((length, columns), jnp.float32)
    for tap in range(FILT):
        d_proj = d_proj + taps[tap] * d_conv[tap : tap + length]
    d_proj = d_proj.astype(jnp.bfloat16)

    copies = jnp.broadcast_to(d_proj[None], (shards, length, columns))
    d_all = lax.all_to_all(copies, "fsdp", 0, 0).reshape(shards * length, columns)
    factors = clip_factors(values, clip_upper, clip_lower)
    d_all, factors = lax.optimization_barrier((d_all, factors))
    d_clipped = lax.dot_general(
        inputs, d_all, (((0,), (0,)), ((), ())), preferred_element_type=jnp.float32
    )
    grad_up, grad_low = soft_clip_grads(factors, d_clipped)
    grad_upper, grad_lower = sum_over_ctx(grad_up), sum_over_ctx(grad_low)
    return (grad_upper, grad_lower)


def solution(mesh):
    return jax.shard_map(
        on_device,
        mesh=mesh,
        in_specs=(
            P(("parts", "fsdp"), "ctx", None, "seq"),
            P("fsdp", "seq"),
            P(("parts", "fsdp"), "seq"),
            P(("parts", "fsdp"), "seq"),
            P("seq", None),
            P(("parts", "fsdp"), "ctx", None, "seq"),
            P(("parts", "fsdp"), "ctx", None, "seq"),
        ),
        out_specs=(P(("parts", "fsdp"), "seq"), P(("parts", "fsdp"), "seq")),
        check_vma=False,
    )
```

```python
import jax
import jax.numpy as jnp
from jax import lax
from jax.sharding import PartitionSpec as P

FILT = 7
CGROUP = 16


def from_behind(value, axis, by):
    devices = lax.axis_size(axis)
    pairs = [(i, i + by) for i in range(devices) if 0 <= i + by < devices]
    return lax.ppermute(value, axis, pairs)


def clip_bounds(values, upper_logit, lower_logit):
    rows = values.shape[0]
    groups = upper_logit.shape[0]
    blocks = values.reshape(groups, rows // groups, values.shape[1])
    amax = jnp.max(jnp.abs(blocks.astype(jnp.bfloat16)), axis=1).astype(jnp.float32) + 1e-06
    upper = jax.nn.sigmoid(upper_logit) * amax
    lower = -jax.nn.sigmoid(lower_logit) * amax
    center = ((upper + lower) * 0.5)[:, None, :]
    radius = ((upper - lower) * 0.5)[:, None, :]
    return blocks, amax, center, radius


def soft_clip(values, upper_logit, lower_logit):
    blocks, _, center, radius = clip_bounds(values, upper_logit, lower_logit)
    clipped = center + radius * jnp.tanh((blocks - center) * (1.0 / radius))
    return clipped.reshape(values.shape)


def soft_clip_grads(values, upper_logit, lower_logit, d_clipped):
    blocks, amax, center, radius = clip_bounds(values, upper_logit, lower_logit)
    z = (blocks - center) * (1.0 / radius)
    t = jnp.tanh(z)
    square = t * t
    slope = t - (1.0 - square) * z
    grouped = d_clipped.reshape(blocks.shape)
    toward_upper = jnp.sum(grouped * (square + slope), axis=1)
    toward_lower = jnp.sum(grouped * (square - slope), axis=1)
    up = jax.nn.sigmoid(upper_logit)
    low = jax.nn.sigmoid(lower_logit)
    grad_up = toward_upper * (0.5 * up * (1.0 - up) * amax)
    grad_low = toward_lower * (-0.5 * low * (1.0 - low) * amax)
    return grad_up, grad_low


def gather_features(local_rows):
    devices = lax.axis_size("seq")
    if devices != 2:
        return lax.all_gather(local_rows, "seq", axis=1, tiled=True)
    other = lax.ppermute(local_rows, "seq", [(0, 1), (1, 0)])
    first = lax.axis_index("seq") == 0
    return jnp.where(
        first,
        jnp.concatenate([local_rows, other], axis=1),
        jnp.concatenate([other, local_rows], axis=1),
    )


def rows_of_block(local_rows, shards, rows, quant):
    devices = lax.axis_size("seq")
    length = local_rows.shape[0]
    if devices != 2 or length % 2:
        features, quant = lax.optimization_barrier((gather_features(local_rows), quant))
        pieces = features.reshape(length, shards, rows).transpose(1, 0, 2)
        return [(lax.all_to_all(pieces, "fsdp", 0, 0), 0)], quant
    half = length // 2
    first = lax.axis_index("seq") == 0
    wanted_by_other = lax.dynamic_slice_in_dim(local_rows, jnp.where(first, half, 0), half, 0)
    kept = lax.dynamic_slice_in_dim(local_rows, jnp.where(first, 0, half), half, 0)
    other = lax.ppermute(wanted_by_other, "seq", [(0, 1), (1, 0)])
    other, quant = lax.optimization_barrier((other, quant))
    features = jnp.where(
        first, jnp.concatenate([kept, other], axis=1), jnp.concatenate([other, kept], axis=1)
    )
    pieces = features.reshape(half, shards, rows).transpose(1, 0, 2)
    own_half = lax.all_to_all(pieces, "fsdp", 0, 0)
    other_half = lax.ppermute(own_half, "seq", [(0, 1), (1, 0)])
    own_at = jnp.where(first, 0, half)
    return [(own_half, own_at), (other_half, half - own_at)], quant


def reduce_partial(partial, me):
    shards = partial.shape[0]
    received = lax.all_to_all(partial.astype(jnp.float16), "fsdp", 0, 0).astype(jnp.float32)
    others = jnp.where((jnp.arange(shards) == me)[:, None, None], 0.0, received)
    own = lax.dynamic_index_in_dim(partial, me, 0, keepdims=False)
    return own + jnp.sum(others, axis=0)


def ring_gather(value, axis):
    devices = lax.axis_size(axis)
    me = lax.axis_index(axis)
    gathered = jnp.zeros((devices,) + value.shape, value.dtype)
    gathered = lax.dynamic_update_index_in_dim(gathered, value, me, 0)
    for shift in range(1, devices):
        block = lax.ppermute(value, axis, [(i, (i + shift) % devices) for i in range(devices)])
        gathered = lax.dynamic_update_index_in_dim(gathered, block, (me + devices - shift) % devices, 0)
    return gathered


def sum_over_ctx(value):
    devices = lax.axis_size("ctx")
    if devices != 2:
        return lax.psum(value, "ctx")
    return value + lax.ppermute(value, "ctx", [(0, 1), (1, 0)])


def on_device(hidden_in, weight, clip_upper, clip_lower, filters, gate, target):
    shards = lax.axis_size("fsdp")
    width = hidden_in.shape[-1]
    local_rows = hidden_in.reshape(-1, width)
    length = local_rows.shape[0]
    rows, columns = weight.shape
    values = weight.astype(jnp.float32)
    quant = soft_clip(values, clip_upper, clip_lower).astype(jnp.bfloat16)
    pieces, quant = rows_of_block(local_rows, shards, rows, quant)
    me = lax.axis_index("fsdp")
    proj = jnp.zeros((length, columns), jnp.float32)
    mine = jnp.zeros((shards, length, rows), local_rows.dtype)
    for piece, at in pieces:
        count = piece.shape[1]
        flat = piece.reshape(shards * count, rows)
        partial = jnp.dot(flat, quant, preferred_element_type=jnp.float32).reshape(shards, count, columns)
        proj = lax.dynamic_update_slice_in_dim(proj, reduce_partial(partial, me), at, 0)
        mine = lax.dynamic_update_slice_in_dim(mine, piece, at, 1)
    proj = proj.astype(jnp.bfloat16)
    inputs = mine.reshape(shards * length, rows)

    taps = jnp.repeat(filters, CGROUP, axis=0).T
    pad = FILT - 1
    previous = from_behind(proj[length - pad :], "ctx", 1)
    upcoming = from_behind(proj[:pad], "ctx", -1)
    gates_in = gate.reshape(length, columns)
    wanted_in = target.reshape(length, columns)
    gates_next = from_behind(gates_in[:pad], "ctx", -1)
    wanted_next = from_behind(wanted_in[:pad], "ctx", -1)
    padded = jnp.concatenate([previous, proj, upcoming], axis=0).astype(jnp.float32)
    extent = length + pad
    conv = jnp.zeros((extent, columns), jnp.float32)
    for tap in range(FILT):
        conv = conv + taps[tap] * padded[pad - tap : pad - tap + extent]
    gates = jnp.concatenate([gates_in, gates_next], axis=0).astype(jnp.float32)
    wanted = jnp.concatenate([wanted_in, wanted_next], axis=0).astype(jnp.float32)
    total_tokens = lax.axis_size("fsdp") * lax.axis_size("ctx") * length
    scale = 1024.0 / jnp.sqrt(jnp.float32(total_tokens))
    d_conv = scale * (gates * conv - wanted) * gates
    d_proj = jnp.zeros((length, columns), jnp.float32)
    for tap in range(FILT):
        d_proj = d_proj + taps[tap] * d_conv[tap : tap + length]
    d_proj = d_proj.astype(jnp.bfloat16)

    d_all = ring_gather(d_proj, "fsdp").reshape(shards * length, columns)
    d_clipped = lax.dot_general(
        inputs, d_all, (((0,), (0,)), ((), ())), preferred_element_type=jnp.float32
    )
    grad_up, grad_low = soft_clip_grads(values, clip_upper, clip_lower, d_clipped)
    grad_upper, grad_lower = sum_over_ctx(grad_up), sum_over_ctx(grad_low)
    return (grad_upper, grad_lower)


def solution(mesh):
    return jax.shard_map(
        on_device,
        mesh=mesh,
        in_specs=(
            P(("parts", "fsdp"), "ctx", None, "seq"),
            P("fsdp", "seq"),
            P(("parts", "fsdp"), "seq"),
            P(("parts", "fsdp"), "seq"),
            P("seq", None),
            P(("parts", "fsdp"), "ctx", None, "seq"),
            P(("parts", "fsdp"), "ctx", None, "seq"),
        ),
        out_specs=(P(("parts", "fsdp"), "seq"), P(("parts", "fsdp"), "seq")),
        check_vma=False,
    )
```

```python
import jax
import jax.numpy as jnp
from jax import lax
from jax.sharding import PartitionSpec as P

FILT = 7
CGROUP = 16


def from_behind(value, axis, by):
    devices = lax.axis_size(axis)
    pairs = [(i, i + by) for i in range(devices) if 0 <= i + by < devices]
    return lax.ppermute(value, axis, pairs)


def clip_bounds(values, upper_logit, lower_logit):
    rows = values.shape[0]
    groups = upper_logit.shape[0]
    blocks = values.reshape(groups, rows // groups, values.shape[1])
    amax = jnp.max(jnp.abs(blocks.astype(jnp.bfloat16)), axis=1).astype(jnp.float32) + 1e-06
    upper = jax.nn.sigmoid(upper_logit) * amax
    lower = -jax.nn.sigmoid(lower_logit) * amax
    center = ((upper + lower) * 0.5)[:, None, :]
    radius = ((upper - lower) * 0.5)[:, None, :]
    return blocks, amax, center, radius


def soft_clip(values, upper_logit, lower_logit):
    blocks, _, center, radius = clip_bounds(values, upper_logit, lower_logit)
    clipped = center + radius * jnp.tanh((blocks - center) * (1.0 / radius))
    return clipped.reshape(values.shape)


def soft_clip_grads(values, upper_logit, lower_logit, d_clipped):
    blocks, amax, center, radius = clip_bounds(values, upper_logit, lower_logit)
    z = (blocks - center) * (1.0 / radius)
    t = jnp.tanh(z)
    square = t * t
    slope = t - (1.0 - square) * z
    grouped = d_clipped.reshape(blocks.shape)
    toward_upper = jnp.sum(grouped * (square + slope), axis=1)
    toward_lower = jnp.sum(grouped * (square - slope), axis=1)
    up = jax.nn.sigmoid(upper_logit)
    low = jax.nn.sigmoid(lower_logit)
    grad_up = toward_upper * (0.5 * up * (1.0 - up) * amax)
    grad_low = toward_lower * (-0.5 * low * (1.0 - low) * amax)
    return grad_up, grad_low


def gather_features(local_rows):
    devices = lax.axis_size("seq")
    if devices != 2:
        return lax.all_gather(local_rows, "seq", axis=1, tiled=True)
    other = lax.ppermute(local_rows, "seq", [(0, 1), (1, 0)])
    first = lax.axis_index("seq") == 0
    return jnp.where(
        first,
        jnp.concatenate([local_rows, other], axis=1),
        jnp.concatenate([other, local_rows], axis=1),
    )


def rows_of_block(local_rows, shards, rows, quant):
    devices = lax.axis_size("seq")
    length = local_rows.shape[0]
    if devices != 2 or length % 2:
        features, quant = lax.optimization_barrier((gather_features(local_rows), quant))
        pieces = features.reshape(length, shards, rows).transpose(1, 0, 2)
        return [(lax.all_to_all(pieces, "fsdp", 0, 0), 0)], quant
    half = length // 2
    first = lax.axis_index("seq") == 0
    wanted_by_other = lax.dynamic_slice_in_dim(local_rows, jnp.where(first, half, 0), half, 0)
    kept = lax.dynamic_slice_in_dim(local_rows, jnp.where(first, 0, half), half, 0)
    other = lax.ppermute(wanted_by_other, "seq", [(0, 1), (1, 0)])
    other, quant = lax.optimization_barrier((other, quant))
    features = jnp.where(
        first, jnp.concatenate([kept, other], axis=1), jnp.concatenate([other, kept], axis=1)
    )
    pieces = features.reshape(half, shards, rows).transpose(1, 0, 2)
    own_half = ring_all_to_all(pieces, "fsdp")
    other_half = lax.ppermute(own_half, "seq", [(0, 1), (1, 0)])
    own_at = jnp.where(first, 0, half)
    return [(own_half, own_at), (other_half, half - own_at)], quant


def reduce_partial(partial, me):
    shards = partial.shape[0]
    received = ring_all_to_all(partial.astype(jnp.float16), "fsdp").astype(jnp.float32)
    others = jnp.where((jnp.arange(shards) == me)[:, None, None], 0.0, received)
    own = lax.dynamic_index_in_dim(partial, me, 0, keepdims=False)
    return own + jnp.sum(others, axis=0)


def ring_gather(value, axis):
    devices = lax.axis_size(axis)
    me = lax.axis_index(axis)
    gathered = jnp.zeros((devices,) + value.shape, value.dtype)
    gathered = lax.dynamic_update_index_in_dim(gathered, value, me, 0)
    for shift in range(1, devices):
        block = lax.ppermute(value, axis, [(i, (i + shift) % devices) for i in range(devices)])
        gathered = lax.dynamic_update_index_in_dim(gathered, block, (me + devices - shift) % devices, 0)
    return gathered


def ring_all_to_all(pieces, axis):
    devices = lax.axis_size(axis)
    me = lax.axis_index(axis)
    received = jnp.zeros_like(pieces)
    received = lax.dynamic_update_index_in_dim(
        received, lax.dynamic_index_in_dim(pieces, me, 0, keepdims=False), me, 0
    )
    for shift in range(1, devices):
        outgoing = lax.dynamic_index_in_dim(pieces, (me + shift) % devices, 0, keepdims=False)
        block = lax.ppermute(outgoing, axis, [(i, (i + shift) % devices) for i in range(devices)])
        received = lax.dynamic_update_index_in_dim(received, block, (me + devices - shift) % devices, 0)
    return received


def sum_over_ctx(value):
    devices = lax.axis_size("ctx")
    if devices != 2:
        return lax.psum(value, "ctx")
    return value + lax.ppermute(value, "ctx", [(0, 1), (1, 0)])


def on_device(hidden_in, weight, clip_upper, clip_lower, filters, gate, target):
    shards = lax.axis_size("fsdp")
    width = hidden_in.shape[-1]
    local_rows = hidden_in.reshape(-1, width)
    length = local_rows.shape[0]
    rows, columns = weight.shape
    values = weight.astype(jnp.float32)
    quant = soft_clip(values, clip_upper, clip_lower).astype(jnp.bfloat16)
    pieces, quant = rows_of_block(local_rows, shards, rows, quant)
    me = lax.axis_index("fsdp")
    proj = jnp.zeros((length, columns), jnp.float32)
    mine = jnp.zeros((shards, length, rows), local_rows.dtype)
    for piece, at in pieces:
        count = piece.shape[1]
        flat = piece.reshape(shards * count, rows)
        partial = jnp.dot(flat, quant, preferred_element_type=jnp.float32).reshape(shards, count, columns)
        proj = lax.dynamic_update_slice_in_dim(proj, reduce_partial(partial, me), at, 0)
        mine = lax.dynamic_update_slice_in_dim(mine, piece, at, 1)
    proj = proj.astype(jnp.bfloat16)
    inputs = mine.reshape(shards * length, rows)

    taps = jnp.repeat(filters, CGROUP, axis=0).T
    pad = FILT - 1
    previous = from_behind(proj[length - pad :], "ctx", 1)
    upcoming = from_behind(proj[:pad], "ctx", -1)
    gates_in = gate.reshape(length, columns)
    wanted_in = target.reshape(length, columns)
    gates_next = from_behind(gates_in[:pad], "ctx", -1)
    wanted_next = from_behind(wanted_in[:pad], "ctx", -1)
    padded = jnp.concatenate([previous, proj, upcoming], axis=0).astype(jnp.float32)
    extent = length + pad
    conv = jnp.zeros((extent, columns), jnp.float32)
    for tap in range(FILT):
        conv = conv + taps[tap] * padded[pad - tap : pad - tap + extent]
    gates = jnp.concatenate([gates_in, gates_next], axis=0).astype(jnp.float32)
    wanted = jnp.concatenate([wanted_in, wanted_next], axis=0).astype(jnp.float32)
    total_tokens = lax.axis_size("fsdp") * lax.axis_size("ctx") * length
    scale = 1024.0 / jnp.sqrt(jnp.float32(total_tokens))
    d_conv = scale * (gates * conv - wanted) * gates
    d_proj = jnp.zeros((length, columns), jnp.float32)
    for tap in range(FILT):
        d_proj = d_proj + taps[tap] * d_conv[tap : tap + length]
    d_proj = d_proj.astype(jnp.bfloat16)

    d_all = ring_gather(d_proj, "fsdp").reshape(shards * length, columns)
    d_clipped = lax.dot_general(
        inputs, d_all, (((0,), (0,)), ((), ())), preferred_element_type=jnp.float32
    )
    grad_up, grad_low = soft_clip_grads(values, clip_upper, clip_lower, d_clipped)
    grad_upper, grad_lower = sum_over_ctx(grad_up), sum_over_ctx(grad_low)
    return (grad_upper, grad_lower)


def solution(mesh):
    return jax.shard_map(
        on_device,
        mesh=mesh,
        in_specs=(
            P(("parts", "fsdp"), "ctx", None, "seq"),
            P("fsdp", "seq"),
            P(("parts", "fsdp"), "seq"),
            P(("parts", "fsdp"), "seq"),
            P("seq", None),
            P(("parts", "fsdp"), "ctx", None, "seq"),
            P(("parts", "fsdp"), "ctx", None, "seq"),
        ),
        out_specs=(P(("parts", "fsdp"), "seq"), P(("parts", "fsdp"), "seq")),
        check_vma=False,
    )
```

```python
import jax
import jax.numpy as jnp
from jax import lax
from jax.sharding import PartitionSpec as P

FILT = 7
CGROUP = 16


def from_behind(value, axis, by):
    devices = lax.axis_size(axis)
    pairs = [(i, i + by) for i in range(devices) if 0 <= i + by < devices]
    return lax.ppermute(value, axis, pairs)


def clip_bounds(values, upper_logit, lower_logit):
    rows = values.shape[0]
    groups = upper_logit.shape[0]
    blocks = values.reshape(groups, rows // groups, values.shape[1])
    amax = jnp.max(jnp.abs(blocks.astype(jnp.bfloat16)), axis=1).astype(jnp.float32) + 1e-06
    upper = jax.nn.sigmoid(upper_logit) * amax
    lower = -jax.nn.sigmoid(lower_logit) * amax
    center = ((upper + lower) * 0.5)[:, None, :]
    radius = ((upper - lower) * 0.5)[:, None, :]
    return blocks, amax, center, radius


def soft_clip(values, upper_logit, lower_logit):
    blocks, _, center, radius = clip_bounds(values, upper_logit, lower_logit)
    clipped = center + radius * jnp.tanh((blocks - center) * (1.0 / radius))
    return clipped.reshape(values.shape)


def soft_clip_grads(values, upper_logit, lower_logit, d_clipped):
    blocks, amax, center, radius = clip_bounds(values, upper_logit, lower_logit)
    z = (blocks - center) * (1.0 / radius)
    t = jnp.tanh(z)
    square = t * t
    slope = t - (1.0 - square) * z
    grouped = d_clipped.reshape(blocks.shape)
    toward_upper = jnp.sum(grouped * (square + slope), axis=1)
    toward_lower = jnp.sum(grouped * (square - slope), axis=1)
    up = jax.nn.sigmoid(upper_logit)
    low = jax.nn.sigmoid(lower_logit)
    grad_up = toward_upper * (0.5 * up * (1.0 - up) * amax)
    grad_low = toward_lower * (-0.5 * low * (1.0 - low) * amax)
    return grad_up, grad_low


def gather_features(local_rows):
    devices = lax.axis_size("seq")
    if devices != 2:
        return lax.all_gather(local_rows, "seq", axis=1, tiled=True)
    other = lax.ppermute(local_rows, "seq", [(0, 1), (1, 0)])
    first = lax.axis_index("seq") == 0
    return jnp.where(
        first,
        jnp.concatenate([local_rows, other], axis=1),
        jnp.concatenate([other, local_rows], axis=1),
    )


def rows_of_block(local_rows, shards, rows, quant):
    devices = lax.axis_size("seq")
    length = local_rows.shape[0]
    if devices != 2 or length % 2:
        features, quant = lax.optimization_barrier((gather_features(local_rows), quant))
        pieces = features.reshape(length, shards, rows).transpose(1, 0, 2)
        return [(lax.all_to_all(pieces, "fsdp", 0, 0), 0)], quant
    half = length // 2
    first = lax.axis_index("seq") == 0
    wanted_by_other = lax.dynamic_slice_in_dim(local_rows, jnp.where(first, half, 0), half, 0)
    kept = lax.dynamic_slice_in_dim(local_rows, jnp.where(first, 0, half), half, 0)
    other = lax.ppermute(wanted_by_other, "seq", [(0, 1), (1, 0)])
    other, quant = lax.optimization_barrier((other, quant))
    features = jnp.where(
        first, jnp.concatenate([kept, other], axis=1), jnp.concatenate([other, kept], axis=1)
    )
    pieces = features.reshape(half, shards, rows).transpose(1, 0, 2)
    own_half = ring_all_to_all(pieces, "fsdp")
    other_half = lax.ppermute(own_half, "seq", [(0, 1), (1, 0)])
    own_at = jnp.where(first, 0, half)
    return [(own_half, own_at), (other_half, half - own_at)], quant


def reduce_partial(partial, me):
    shards = partial.shape[0]
    received = lax.all_to_all(partial.astype(jnp.float16), "fsdp", 0, 0).astype(jnp.float32)
    others = jnp.where((jnp.arange(shards) == me)[:, None, None], 0.0, received)
    own = lax.dynamic_index_in_dim(partial, me, 0, keepdims=False)
    return own + jnp.sum(others, axis=0)


def ring_gather(value, axis):
    devices = lax.axis_size(axis)
    me = lax.axis_index(axis)
    gathered = jnp.zeros((devices,) + value.shape, value.dtype)
    gathered = lax.dynamic_update_index_in_dim(gathered, value, me, 0)
    for shift in range(1, devices):
        block = lax.ppermute(value, axis, [(i, (i + shift) % devices) for i in range(devices)])
        gathered = lax.dynamic_update_index_in_dim(gathered, block, (me + devices - shift) % devices, 0)
    return gathered


def ring_all_to_all(pieces, axis):
    devices = lax.axis_size(axis)
    me = lax.axis_index(axis)
    received = jnp.zeros_like(pieces)
    received = lax.dynamic_update_index_in_dim(
        received, lax.dynamic_index_in_dim(pieces, me, 0, keepdims=False), me, 0
    )
    for shift in range(1, devices):
        outgoing = lax.dynamic_index_in_dim(pieces, (me + shift) % devices, 0, keepdims=False)
        block = lax.ppermute(outgoing, axis, [(i, (i + shift) % devices) for i in range(devices)])
        received = lax.dynamic_update_index_in_dim(received, block, (me + devices - shift) % devices, 0)
    return received


def sum_over_ctx(value):
    devices = lax.axis_size("ctx")
    if devices != 2:
        return lax.psum(value, "ctx")
    return value + lax.ppermute(value, "ctx", [(0, 1), (1, 0)])


def on_device(hidden_in, weight, clip_upper, clip_lower, filters, gate, target):
    shards = lax.axis_size("fsdp")
    width = hidden_in.shape[-1]
    local_rows = hidden_in.reshape(-1, width)
    length = local_rows.shape[0]
    rows, columns = weight.shape
    values = weight.astype(jnp.float32)
    quant = soft_clip(values, clip_upper, clip_lower).astype(jnp.bfloat16)
    pieces, quant = rows_of_block(local_rows, shards, rows, quant)
    me = lax.axis_index("fsdp")
    proj = jnp.zeros((length, columns), jnp.float32)
    mine = jnp.zeros((shards, length, rows), local_rows.dtype)
    for piece, at in pieces:
        count = piece.shape[1]
        flat = piece.reshape(shards * count, rows)
        partial = jnp.dot(flat, quant, preferred_element_type=jnp.float32).reshape(shards, count, columns)
        proj = lax.dynamic_update_slice_in_dim(proj, reduce_partial(partial, me), at, 0)
        mine = lax.dynamic_update_slice_in_dim(mine, piece, at, 1)
    proj = proj.astype(jnp.bfloat16)
    inputs = mine.reshape(shards * length, rows)

    taps = jnp.repeat(filters, CGROUP, axis=0).T
    pad = FILT - 1
    previous = from_behind(proj[length - pad :], "ctx", 1)
    upcoming = from_behind(proj[:pad], "ctx", -1)
    gates_in = gate.reshape(length, columns)
    wanted_in = target.reshape(length, columns)
    gates_next = from_behind(gates_in[:pad], "ctx", -1)
    wanted_next = from_behind(wanted_in[:pad], "ctx", -1)
    padded = jnp.concatenate([previous, proj, upcoming], axis=0).astype(jnp.float32)
    extent = length + pad
    conv = jnp.zeros((extent, columns), jnp.float32)
    for tap in range(FILT):
        conv = conv + taps[tap] * padded[pad - tap : pad - tap + extent]
    gates = jnp.concatenate([gates_in, gates_next], axis=0).astype(jnp.float32)
    wanted = jnp.concatenate([wanted_in, wanted_next], axis=0).astype(jnp.float32)
    total_tokens = lax.axis_size("fsdp") * lax.axis_size("ctx") * length
    scale = 1024.0 / jnp.sqrt(jnp.float32(total_tokens))
    d_conv = scale * (gates * conv - wanted) * gates
    d_proj = jnp.zeros((length, columns), jnp.float32)
    for tap in range(FILT):
        d_proj = d_proj + taps[tap] * d_conv[tap : tap + length]
    d_proj = d_proj.astype(jnp.bfloat16)

    d_all = ring_gather(d_proj, "fsdp").reshape(shards * length, columns)
    d_clipped = lax.dot_general(
        inputs, d_all, (((0,), (0,)), ((), ())), preferred_element_type=jnp.float32
    )
    grad_up, grad_low = soft_clip_grads(values, clip_upper, clip_lower, d_clipped)
    grad_upper, grad_lower = sum_over_ctx(grad_up), sum_over_ctx(grad_low)
    return (grad_upper, grad_lower)


def solution(mesh):
    return jax.shard_map(
        on_device,
        mesh=mesh,
        in_specs=(
            P(("parts", "fsdp"), "ctx", None, "seq"),
            P("fsdp", "seq"),
            P(("parts", "fsdp"), "seq"),
            P(("parts", "fsdp"), "seq"),
            P("seq", None),
            P(("parts", "fsdp"), "ctx", None, "seq"),
            P(("parts", "fsdp"), "ctx", None, "seq"),
        ),
        out_specs=(P(("parts", "fsdp"), "seq"), P(("parts", "fsdp"), "seq")),
        check_vma=False,
    )
```

```python
import jax
import jax.numpy as jnp
from jax import lax
from jax.sharding import PartitionSpec as P

FILT = 7
CGROUP = 16


def from_behind(value, axis, by):
    devices = lax.axis_size(axis)
    pairs = [(i, i + by) for i in range(devices) if 0 <= i + by < devices]
    return lax.ppermute(value, axis, pairs)


def clip_bounds(values, upper_logit, lower_logit):
    rows = values.shape[0]
    groups = upper_logit.shape[0]
    blocks = values.reshape(groups, rows // groups, values.shape[1])
    amax = jnp.max(jnp.abs(blocks.astype(jnp.bfloat16)), axis=1).astype(jnp.float32) + 1e-06
    upper = jax.nn.sigmoid(upper_logit) * amax
    lower = -jax.nn.sigmoid(lower_logit) * amax
    center = ((upper + lower) * 0.5)[:, None, :]
    radius = ((upper - lower) * 0.5)[:, None, :]
    return blocks, amax, center, radius


def soft_clip(values, upper_logit, lower_logit):
    blocks, _, center, radius = clip_bounds(values, upper_logit, lower_logit)
    clipped = center + radius * jnp.tanh((blocks - center) * (1.0 / radius))
    return clipped.reshape(values.shape)


def soft_clip_grads(values, upper_logit, lower_logit, d_clipped):
    blocks, amax, center, radius = clip_bounds(values, upper_logit, lower_logit)
    z = (blocks - center) * (1.0 / radius)
    t = jnp.tanh(z)
    square = t * t
    slope = t - (1.0 - square) * z
    grouped = d_clipped.reshape(blocks.shape)
    toward_upper = jnp.sum(grouped * (square + slope), axis=1)
    toward_lower = jnp.sum(grouped * (square - slope), axis=1)
    up = jax.nn.sigmoid(upper_logit)
    low = jax.nn.sigmoid(lower_logit)
    grad_up = toward_upper * (0.5 * up * (1.0 - up) * amax)
    grad_low = toward_lower * (-0.5 * low * (1.0 - low) * amax)
    return grad_up, grad_low


def gather_features(local_rows):
    devices = lax.axis_size("seq")
    if devices != 2:
        return lax.all_gather(local_rows, "seq", axis=1, tiled=True)
    other = lax.ppermute(local_rows, "seq", [(0, 1), (1, 0)])
    first = lax.axis_index("seq") == 0
    return jnp.where(
        first,
        jnp.concatenate([local_rows, other], axis=1),
        jnp.concatenate([other, local_rows], axis=1),
    )


def rows_of_block(local_rows, shards, rows, quant):
    devices = lax.axis_size("seq")
    length = local_rows.shape[0]
    if devices != 2 or length % 2:
        features, quant = lax.optimization_barrier((gather_features(local_rows), quant))
        pieces = features.reshape(length, shards, rows).transpose(1, 0, 2)
        return [(lax.all_to_all(pieces, "fsdp", 0, 0), 0)], quant
    half = length // 2
    first = lax.axis_index("seq") == 0
    wanted_by_other = lax.dynamic_slice_in_dim(local_rows, jnp.where(first, half, 0), half, 0)
    kept = lax.dynamic_slice_in_dim(local_rows, jnp.where(first, 0, half), half, 0)
    other = lax.ppermute(wanted_by_other, "seq", [(0, 1), (1, 0)])
    other, quant = lax.optimization_barrier((other, quant))
    features = jnp.where(
        first, jnp.concatenate([kept, other], axis=1), jnp.concatenate([other, kept], axis=1)
    )
    pieces = features.reshape(half, shards, rows).transpose(1, 0, 2)
    own_half = lax.all_to_all(pieces, "fsdp", 0, 0)
    other_half = lax.ppermute(own_half, "seq", [(0, 1), (1, 0)])
    own_at = jnp.where(first, 0, half)
    return [(own_half, own_at), (other_half, half - own_at)], quant


def reduce_partial(partial, me):
    shards = partial.shape[0]
    received = lax.all_to_all(partial.astype(jnp.float16), "fsdp", 0, 0).astype(jnp.float32)
    others = jnp.where((jnp.arange(shards) == me)[:, None, None], 0.0, received)
    own = lax.dynamic_index_in_dim(partial, me, 0, keepdims=False)
    return own + jnp.sum(others, axis=0)


def ring_gather(value, axis):
    devices = lax.axis_size(axis)
    blocks = [value]
    for shift in range(1, devices):
        blocks.append(lax.ppermute(value, axis, [(i, (i + shift) % devices) for i in range(devices)]))
    return jnp.stack(blocks)


def in_shift_order(pieces, axis):
    devices = lax.axis_size(axis)
    me = lax.axis_index(axis)
    return jnp.stack(
        [lax.dynamic_index_in_dim(pieces, (me + devices - shift) % devices, 0, keepdims=False) for shift in range(devices)]
    )


def sum_over_ctx(first, second):
    devices = lax.axis_size("ctx")
    if devices != 2:
        return lax.psum((first, second), "ctx")
    both = jnp.stack([first, second])
    total = both + lax.ppermute(both, "ctx", [(0, 1), (1, 0)])
    return total[0], total[1]


def on_device(hidden_in, weight, clip_upper, clip_lower, filters, gate, target):
    shards = lax.axis_size("fsdp")
    width = hidden_in.shape[-1]
    local_rows = hidden_in.reshape(-1, width)
    length = local_rows.shape[0]
    rows, columns = weight.shape
    values = weight.astype(jnp.float32)
    quant = soft_clip(values, clip_upper, clip_lower).astype(jnp.bfloat16)
    pieces, quant = rows_of_block(local_rows, shards, rows, quant)
    me = lax.axis_index("fsdp")
    proj = jnp.zeros((length, columns), jnp.float32)
    mine = jnp.zeros((shards, length, rows), local_rows.dtype)
    for piece, at in pieces:
        count = piece.shape[1]
        flat = piece.reshape(shards * count, rows)
        partial = jnp.dot(flat, quant, preferred_element_type=jnp.float32).reshape(shards, count, columns)
        proj = lax.dynamic_update_slice_in_dim(proj, reduce_partial(partial, me), at, 0)
        mine = lax.dynamic_update_slice_in_dim(mine, piece, at, 1)
    proj = proj.astype(jnp.bfloat16)
    inputs = mine.reshape(shards * length, rows)

    taps = jnp.repeat(filters, CGROUP, axis=0).T
    pad = FILT - 1
    previous = from_behind(proj[length - pad :], "ctx", 1)
    upcoming = from_behind(proj[:pad], "ctx", -1)
    gates_in = gate.reshape(length, columns)
    wanted_in = target.reshape(length, columns)
    gates_next = from_behind(gates_in[:pad], "ctx", -1)
    wanted_next = from_behind(wanted_in[:pad], "ctx", -1)
    padded = jnp.concatenate([previous, proj, upcoming], axis=0).astype(jnp.float32)
    extent = length + pad
    conv = jnp.zeros((extent, columns), jnp.float32)
    for tap in range(FILT):
        conv = conv + taps[tap] * padded[pad - tap : pad - tap + extent]
    gates = jnp.concatenate([gates_in, gates_next], axis=0).astype(jnp.float32)
    wanted = jnp.concatenate([wanted_in, wanted_next], axis=0).astype(jnp.float32)
    total_tokens = lax.axis_size("fsdp") * lax.axis_size("ctx") * length
    scale = 1024.0 / jnp.sqrt(jnp.float32(total_tokens))
    d_conv = scale * (gates * conv - wanted) * gates
    d_proj = jnp.zeros((length, columns), jnp.float32)
    for tap in range(FILT):
        d_proj = d_proj + taps[tap] * d_conv[tap : tap + length]
    d_proj = d_proj.astype(jnp.bfloat16)

    d_all = ring_gather(d_proj, "fsdp").reshape(shards * length, columns)
    inputs = in_shift_order(mine, "fsdp").reshape(shards * length, rows)
    d_clipped = lax.dot_general(
        inputs, d_all, (((0,), (0,)), ((), ())), preferred_element_type=jnp.float32
    )
    grad_up, grad_low = soft_clip_grads(values, clip_upper, clip_lower, d_clipped)
    grad_upper, grad_lower = sum_over_ctx(grad_up, grad_low)
    return (grad_upper, grad_lower)


def solution(mesh):
    return jax.shard_map(
        on_device,
        mesh=mesh,
        in_specs=(
            P(("parts", "fsdp"), "ctx", None, "seq"),
            P("fsdp", "seq"),
            P(("parts", "fsdp"), "seq"),
            P(("parts", "fsdp"), "seq"),
            P("seq", None),
            P(("parts", "fsdp"), "ctx", None, "seq"),
            P(("parts", "fsdp"), "ctx", None, "seq"),
        ),
        out_specs=(P(("parts", "fsdp"), "seq"), P(("parts", "fsdp"), "seq")),
        check_vma=False,
    )
```

```python
import jax
import jax.numpy as jnp
from jax import lax
from jax.sharding import PartitionSpec as P

FILT = 7
CGROUP = 16


def from_behind(value, axis, by):
    devices = lax.axis_size(axis)
    pairs = [(i, i + by) for i in range(devices) if 0 <= i + by < devices]
    return lax.ppermute(value, axis, pairs)


def clip_bounds(values, upper_logit, lower_logit):
    rows = values.shape[0]
    groups = upper_logit.shape[0]
    blocks = values.reshape(groups, rows // groups, values.shape[1])
    amax = jnp.max(jnp.abs(blocks.astype(jnp.bfloat16)), axis=1).astype(jnp.float32) + 1e-06
    upper = jax.nn.sigmoid(upper_logit) * amax
    lower = -jax.nn.sigmoid(lower_logit) * amax
    center = ((upper + lower) * 0.5)[:, None, :]
    radius = ((upper - lower) * 0.5)[:, None, :]
    return blocks, amax, center, radius


def soft_clip(values, upper_logit, lower_logit):
    blocks, _, center, radius = clip_bounds(values, upper_logit, lower_logit)
    clipped = center + radius * jnp.tanh((blocks - center) * (1.0 / radius))
    return clipped.reshape(values.shape)


def soft_clip_grads(values, upper_logit, lower_logit, d_clipped):
    blocks, amax, center, radius = clip_bounds(values, upper_logit, lower_logit)
    z = (blocks - center) * (1.0 / radius)
    t = jnp.tanh(z)
    square = t * t
    slope = t - (1.0 - square) * z
    grouped = d_clipped.reshape(blocks.shape)
    toward_upper = jnp.sum(grouped * (square + slope), axis=1)
    toward_lower = jnp.sum(grouped * (square - slope), axis=1)
    up = jax.nn.sigmoid(upper_logit)
    low = jax.nn.sigmoid(lower_logit)
    grad_up = toward_upper * (0.5 * up * (1.0 - up) * amax)
    grad_low = toward_lower * (-0.5 * low * (1.0 - low) * amax)
    return grad_up, grad_low


def gather_features(local_rows):
    devices = lax.axis_size("seq")
    if devices != 2:
        return lax.all_gather(local_rows, "seq", axis=1, tiled=True)
    other = lax.ppermute(local_rows, "seq", [(0, 1), (1, 0)])
    first = lax.axis_index("seq") == 0
    return jnp.where(
        first,
        jnp.concatenate([local_rows, other], axis=1),
        jnp.concatenate([other, local_rows], axis=1),
    )


def rows_of_block(local_rows, shards, rows, quant):
    devices = lax.axis_size("seq")
    length = local_rows.shape[0]
    if devices != 2 or length % 2:
        features, quant = lax.optimization_barrier((gather_features(local_rows), quant))
        pieces = features.reshape(length, shards, rows).transpose(1, 0, 2)
        return [(lax.all_to_all(pieces, "fsdp", 0, 0), 0)], quant
    half = length // 2
    first = lax.axis_index("seq") == 0
    wanted_by_other = lax.dynamic_slice_in_dim(local_rows, jnp.where(first, half, 0), half, 0)
    kept = lax.dynamic_slice_in_dim(local_rows, jnp.where(first, 0, half), half, 0)
    other = lax.ppermute(wanted_by_other, "seq", [(0, 1), (1, 0)])
    other, quant = lax.optimization_barrier((other, quant))
    features = jnp.where(
        first, jnp.concatenate([kept, other], axis=1), jnp.concatenate([other, kept], axis=1)
    )
    pieces = features.reshape(half, shards, rows).transpose(1, 0, 2)
    own_half = lax.all_to_all(pieces, "fsdp", 0, 0)
    other_half = lax.ppermute(own_half, "seq", [(0, 1), (1, 0)])
    own_at = jnp.where(first, 0, half)
    return [(own_half, own_at), (other_half, half - own_at)], quant


def reduce_partial(partial, me):
    shards = partial.shape[0]
    received = lax.all_to_all(partial.astype(jnp.float16), "fsdp", 0, 0).astype(jnp.float32)
    others = jnp.where((jnp.arange(shards) == me)[:, None, None], 0.0, received)
    own = lax.dynamic_index_in_dim(partial, me, 0, keepdims=False)
    return own + jnp.sum(others, axis=0)


def ring_gather(value, axis):
    devices = lax.axis_size(axis)
    me = lax.axis_index(axis)
    gathered = jnp.zeros((devices,) + value.shape, value.dtype)
    gathered = lax.dynamic_update_index_in_dim(gathered, value, me, 0)
    for shift in range(1, devices):
        block = lax.ppermute(value, axis, [(i, (i + shift) % devices) for i in range(devices)])
        gathered = lax.dynamic_update_index_in_dim(gathered, block, (me + devices - shift) % devices, 0)
    return gathered


def sum_over_ctx(first, second):
    devices = lax.axis_size("ctx")
    if devices != 2:
        return lax.psum((first, second), "ctx")
    both = jnp.stack([first, second])
    total = both + lax.ppermute(both, "ctx", [(0, 1), (1, 0)])
    return total[0], total[1]


def on_device(hidden_in, weight, clip_upper, clip_lower, filters, gate, target):
    shards = lax.axis_size("fsdp")
    width = hidden_in.shape[-1]
    local_rows = hidden_in.reshape(-1, width)
    length = local_rows.shape[0]
    rows, columns = weight.shape
    values = weight.astype(jnp.float32)
    quant = soft_clip(values, clip_upper, clip_lower).astype(jnp.bfloat16)
    pieces, quant = rows_of_block(local_rows, shards, rows, quant)
    me = lax.axis_index("fsdp")
    proj = jnp.zeros((length, columns), jnp.float32)
    mine = jnp.zeros((shards, length, rows), local_rows.dtype)
    for piece, at in pieces:
        count = piece.shape[1]
        flat = piece.reshape(shards * count, rows)
        partial = jnp.dot(flat, quant, preferred_element_type=jnp.float32).reshape(shards, count, columns)
        proj = lax.dynamic_update_slice_in_dim(proj, reduce_partial(partial, me), at, 0)
        mine = lax.dynamic_update_slice_in_dim(mine, piece, at, 1)
    proj = proj.astype(jnp.bfloat16)
    inputs = mine.reshape(shards * length, rows)

    taps = jnp.repeat(filters, CGROUP, axis=0).T
    pad = FILT - 1
    previous = from_behind(proj[length - pad :], "ctx", 1)
    upcoming = from_behind(proj[:pad], "ctx", -1)
    gates_in = gate.reshape(length, columns)
    wanted_in = target.reshape(length, columns)
    gates_next = from_behind(gates_in[:pad], "ctx", -1)
    wanted_next = from_behind(wanted_in[:pad], "ctx", -1)
    padded = jnp.concatenate([previous, proj, upcoming], axis=0).astype(jnp.float32)
    extent = length + pad
    conv = jnp.zeros((extent, columns), jnp.float32)
    for tap in range(FILT):
        conv = conv + taps[tap] * padded[pad - tap : pad - tap + extent]
    gates = jnp.concatenate([gates_in, gates_next], axis=0).astype(jnp.float32)
    wanted = jnp.concatenate([wanted_in, wanted_next], axis=0).astype(jnp.float32)
    total_tokens = lax.axis_size("fsdp") * lax.axis_size("ctx") * length
    scale = 1024.0 / jnp.sqrt(jnp.float32(total_tokens))
    d_conv = scale * (gates * conv - wanted) * gates
    d_proj = jnp.zeros((length, columns), jnp.float32)
    for tap in range(FILT):
        d_proj = d_proj + taps[tap] * d_conv[tap : tap + length]
    d_proj = d_proj.astype(jnp.bfloat16)

    d_all = ring_gather(d_proj, "fsdp").reshape(shards * length, columns)
    d_clipped = lax.dot_general(
        inputs, d_all, (((0,), (0,)), ((), ())), preferred_element_type=jnp.float32
    )
    grad_up, grad_low = soft_clip_grads(values, clip_upper, clip_lower, d_clipped)
    grad_upper, grad_lower = sum_over_ctx(grad_up, grad_low)
    return (grad_upper, grad_lower)


def solution(mesh):
    return jax.shard_map(
        on_device,
        mesh=mesh,
        in_specs=(
            P(("parts", "fsdp"), "ctx", None, "seq"),
            P("fsdp", "seq"),
            P(("parts", "fsdp"), "seq"),
            P(("parts", "fsdp"), "seq"),
            P("seq", None),
            P(("parts", "fsdp"), "ctx", None, "seq"),
            P(("parts", "fsdp"), "ctx", None, "seq"),
        ),
        out_specs=(P(("parts", "fsdp"), "seq"), P(("parts", "fsdp"), "seq")),
        check_vma=False,
    )
```

```python
import jax
import jax.numpy as jnp
from jax import lax
from jax.sharding import PartitionSpec as P

FILT = 7
CGROUP = 16


def from_behind(value, axis, by):
    devices = lax.axis_size(axis)
    pairs = [(i, i + by) for i in range(devices) if 0 <= i + by < devices]
    return lax.ppermute(value, axis, pairs)


def clip_bounds(values, upper_logit, lower_logit):
    rows = values.shape[0]
    groups = upper_logit.shape[0]
    blocks = values.reshape(groups, rows // groups, values.shape[1])
    amax = jnp.max(jnp.abs(blocks.astype(jnp.bfloat16)), axis=1).astype(jnp.float32) + 1e-06
    upper = jax.nn.sigmoid(upper_logit) * amax
    lower = -jax.nn.sigmoid(lower_logit) * amax
    center = ((upper + lower) * 0.5)[:, None, :]
    radius = ((upper - lower) * 0.5)[:, None, :]
    return blocks, amax, center, radius


def soft_clip(values, upper_logit, lower_logit):
    blocks, _, center, radius = clip_bounds(values, upper_logit, lower_logit)
    clipped = center + radius * jnp.tanh((blocks - center) * (1.0 / radius))
    return clipped.reshape(values.shape)


def soft_clip_grads(values, upper_logit, lower_logit, d_clipped):
    blocks, amax, center, radius = clip_bounds(values, upper_logit, lower_logit)
    z = (blocks - center) * (1.0 / radius)
    t = jnp.tanh(z)
    square = t * t
    slope = t - (1.0 - square) * z
    grouped = d_clipped.reshape(blocks.shape)
    toward_upper = jnp.sum(grouped * (square + slope), axis=1)
    toward_lower = jnp.sum(grouped * (square - slope), axis=1)
    up = jax.nn.sigmoid(upper_logit)
    low = jax.nn.sigmoid(lower_logit)
    grad_up = toward_upper * (0.5 * up * (1.0 - up) * amax)
    grad_low = toward_lower * (-0.5 * low * (1.0 - low) * amax)
    return grad_up, grad_low


def gather_features(local_rows):
    devices = lax.axis_size("seq")
    if devices != 2:
        return lax.all_gather(local_rows, "seq", axis=1, tiled=True)
    other = lax.ppermute(local_rows, "seq", [(0, 1), (1, 0)])
    first = lax.axis_index("seq") == 0
    return jnp.where(
        first,
        jnp.concatenate([local_rows, other], axis=1),
        jnp.concatenate([other, local_rows], axis=1),
    )


def rows_of_block(local_rows, shards, rows, quant):
    devices = lax.axis_size("seq")
    length = local_rows.shape[0]
    if devices != 2 or length % 2:
        features, quant = lax.optimization_barrier((gather_features(local_rows), quant))
        pieces = features.reshape(length, shards, rows).transpose(1, 0, 2)
        return [(lax.all_to_all(pieces, "fsdp", 0, 0), 0)], quant
    half = length // 2
    first = lax.axis_index("seq") == 0
    wanted_by_other = lax.dynamic_slice_in_dim(local_rows, jnp.where(first, half, 0), half, 0)
    kept = lax.dynamic_slice_in_dim(local_rows, jnp.where(first, 0, half), half, 0)
    other = lax.ppermute(wanted_by_other, "seq", [(0, 1), (1, 0)])
    other, quant = lax.optimization_barrier((other, quant))
    features = jnp.where(
        first, jnp.concatenate([kept, other], axis=1), jnp.concatenate([other, kept], axis=1)
    )
    pieces = features.reshape(half, shards, rows).transpose(1, 0, 2)
    own_half = lax.all_to_all(pieces, "fsdp", 0, 0)
    other_half = lax.ppermute(own_half, "seq", [(0, 1), (1, 0)])
    own_at = jnp.where(first, 0, half)
    return [(own_half, own_at), (other_half, half - own_at)], quant


def reduce_partial(partial, me):
    shards = partial.shape[0]
    received = lax.all_to_all(partial.astype(jnp.float16), "fsdp", 0, 0).astype(jnp.float32)
    others = jnp.where((jnp.arange(shards) == me)[:, None, None], 0.0, received)
    own = lax.dynamic_index_in_dim(partial, me, 0, keepdims=False)
    return own + jnp.sum(others, axis=0)


def ring_gather(value, axis):
    devices = lax.axis_size(axis)
    me = lax.axis_index(axis)
    gathered = jnp.broadcast_to(value[None], (devices,) + value.shape)
    for shift in range(1, devices):
        block = lax.ppermute(value, axis, [(i, (i + shift) % devices) for i in range(devices)])
        gathered = lax.dynamic_update_index_in_dim(gathered, block, (me + devices - shift) % devices, 0)
    return gathered


def sum_over_ctx(first, second):
    devices = lax.axis_size("ctx")
    if devices != 2:
        return lax.psum((first, second), "ctx")
    both = jnp.stack([first, second])
    total = both + lax.ppermute(both, "ctx", [(0, 1), (1, 0)])
    return total[0], total[1]


def on_device(hidden_in, weight, clip_upper, clip_lower, filters, gate, target):
    shards = lax.axis_size("fsdp")
    width = hidden_in.shape[-1]
    local_rows = hidden_in.reshape(-1, width)
    length = local_rows.shape[0]
    rows, columns = weight.shape
    values = weight.astype(jnp.float32)
    quant = soft_clip(values, clip_upper, clip_lower).astype(jnp.bfloat16)
    pieces, quant = rows_of_block(local_rows, shards, rows, quant)
    me = lax.axis_index("fsdp")
    proj = jnp.zeros((length, columns), jnp.float32)
    mine = jnp.zeros((shards, length, rows), local_rows.dtype)
    for piece, at in pieces:
        count = piece.shape[1]
        flat = piece.reshape(shards * count, rows)
        partial = jnp.dot(flat, quant, preferred_element_type=jnp.float32).reshape(shards, count, columns)
        proj = lax.dynamic_update_slice_in_dim(proj, reduce_partial(partial, me), at, 0)
        mine = lax.dynamic_update_slice_in_dim(mine, piece, at, 1)
    proj = proj.astype(jnp.bfloat16)
    inputs = mine.reshape(shards * length, rows)

    taps = jnp.repeat(filters, CGROUP, axis=0).T
    pad = FILT - 1
    previous = from_behind(proj[length - pad :], "ctx", 1)
    upcoming = from_behind(proj[:pad], "ctx", -1)
    gates_in = gate.reshape(length, columns)
    wanted_in = target.reshape(length, columns)
    gates_next = from_behind(gates_in[:pad], "ctx", -1)
    wanted_next = from_behind(wanted_in[:pad], "ctx", -1)
    padded = jnp.concatenate([previous, proj, upcoming], axis=0).astype(jnp.float32)
    extent = length + pad
    conv = jnp.zeros((extent, columns), jnp.float32)
    for tap in range(FILT):
        conv = conv + taps[tap] * padded[pad - tap : pad - tap + extent]
    gates = jnp.concatenate([gates_in, gates_next], axis=0).astype(jnp.float32)
    wanted = jnp.concatenate([wanted_in, wanted_next], axis=0).astype(jnp.float32)
    total_tokens = lax.axis_size("fsdp") * lax.axis_size("ctx") * length
    scale = 1024.0 / jnp.sqrt(jnp.float32(total_tokens))
    d_conv = scale * (gates * conv - wanted) * gates
    d_proj = jnp.zeros((length, columns), jnp.float32)
    for tap in range(FILT):
        d_proj = d_proj + taps[tap] * d_conv[tap : tap + length]
    d_proj = d_proj.astype(jnp.bfloat16)

    d_all = ring_gather(d_proj, "fsdp").reshape(shards * length, columns)
    d_clipped = lax.dot_general(
        inputs, d_all, (((0,), (0,)), ((), ())), preferred_element_type=jnp.float32
    )
    grad_up, grad_low = soft_clip_grads(values, clip_upper, clip_lower, d_clipped)
    grad_upper, grad_lower = sum_over_ctx(grad_up, grad_low)
    return (grad_upper, grad_lower)


def solution(mesh):
    return jax.shard_map(
        on_device,
        mesh=mesh,
        in_specs=(
            P(("parts", "fsdp"), "ctx", None, "seq"),
            P("fsdp", "seq"),
            P(("parts", "fsdp"), "seq"),
            P(("parts", "fsdp"), "seq"),
            P("seq", None),
            P(("parts", "fsdp"), "ctx", None, "seq"),
            P(("parts", "fsdp"), "ctx", None, "seq"),
        ),
        out_specs=(P(("parts", "fsdp"), "seq"), P(("parts", "fsdp"), "seq")),
        check_vma=False,
    )
```

```python
import jax
import jax.numpy as jnp
from jax import lax
from jax.sharding import PartitionSpec as P

FILT = 7
CGROUP = 16


def from_behind(value, axis, by):
    devices = lax.axis_size(axis)
    pairs = [(i, i + by) for i in range(devices) if 0 <= i + by < devices]
    return lax.ppermute(value, axis, pairs)


def clip_bounds(values, upper_logit, lower_logit):
    rows = values.shape[0]
    groups = upper_logit.shape[0]
    blocks = values.reshape(groups, rows // groups, values.shape[1])
    amax = jnp.max(jnp.abs(blocks.astype(jnp.bfloat16)), axis=1).astype(jnp.float32) + 1e-06
    upper = jax.nn.sigmoid(upper_logit) * amax
    lower = -jax.nn.sigmoid(lower_logit) * amax
    center = ((upper + lower) * 0.5)[:, None, :]
    radius = ((upper - lower) * 0.5)[:, None, :]
    return blocks, amax, center, radius


def soft_clip(values, upper_logit, lower_logit):
    blocks, _, center, radius = clip_bounds(values, upper_logit, lower_logit)
    clipped = center + radius * jnp.tanh((blocks - center) * (1.0 / radius))
    return clipped.reshape(values.shape)


def soft_clip_grads(values, upper_logit, lower_logit, d_clipped):
    blocks, amax, center, radius = clip_bounds(values, upper_logit, lower_logit)
    z = (blocks - center) * (1.0 / radius)
    t = jnp.tanh(z)
    square = t * t
    slope = t - (1.0 - square) * z
    grouped = d_clipped.reshape(blocks.shape)
    toward_upper = jnp.sum(grouped * (square + slope), axis=1)
    toward_lower = jnp.sum(grouped * (square - slope), axis=1)
    up = jax.nn.sigmoid(upper_logit)
    low = jax.nn.sigmoid(lower_logit)
    grad_up = toward_upper * (0.5 * up * (1.0 - up) * amax)
    grad_low = toward_lower * (-0.5 * low * (1.0 - low) * amax)
    return grad_up, grad_low


def gather_features(local_rows):
    devices = lax.axis_size("seq")
    if devices != 2:
        return lax.all_gather(local_rows, "seq", axis=1, tiled=True)
    other = lax.ppermute(local_rows, "seq", [(0, 1), (1, 0)])
    first = lax.axis_index("seq") == 0
    return jnp.where(
        first,
        jnp.concatenate([local_rows, other], axis=1),
        jnp.concatenate([other, local_rows], axis=1),
    )


def rows_of_block(local_rows, shards, rows, quant):
    devices = lax.axis_size("seq")
    length = local_rows.shape[0]
    if devices != 2 or length % 2:
        features, quant = lax.optimization_barrier((gather_features(local_rows), quant))
        pieces = features.reshape(length, shards, rows).transpose(1, 0, 2)
        return [(lax.all_to_all(pieces, "fsdp", 0, 0), 0)], quant
    half = length // 2
    first = lax.axis_index("seq") == 0
    wanted_by_other = lax.dynamic_slice_in_dim(local_rows, jnp.where(first, half, 0), half, 0)
    kept = lax.dynamic_slice_in_dim(local_rows, jnp.where(first, 0, half), half, 0)
    other = lax.ppermute(wanted_by_other, "seq", [(0, 1), (1, 0)])
    other, quant = lax.optimization_barrier((other, quant))
    features = jnp.where(
        first, jnp.concatenate([kept, other], axis=1), jnp.concatenate([other, kept], axis=1)
    )
    pieces = features.reshape(half, shards, rows).transpose(1, 0, 2)
    own_half = lax.all_to_all(pieces, "fsdp", 0, 0)
    other_half = lax.ppermute(own_half, "seq", [(0, 1), (1, 0)])
    own_at = jnp.where(first, 0, half)
    return [(own_half, own_at), (other_half, half - own_at)], quant


def reduce_partial(partial, me):
    shards = partial.shape[0]
    received = lax.all_to_all(partial.astype(jnp.float16), "fsdp", 0, 0).astype(jnp.float32)
    others = jnp.where((jnp.arange(shards) == me)[:, None, None], 0.0, received)
    own = lax.dynamic_index_in_dim(partial, me, 0, keepdims=False)
    return own + jnp.sum(others, axis=0)


def ring_gather(value, axis):
    devices = lax.axis_size(axis)
    me = lax.axis_index(axis)
    gathered = jnp.broadcast_to(value[None], (devices,) + value.shape)
    for shift in range(1, devices):
        block = lax.ppermute(value, axis, [(i, (i + shift) % devices) for i in range(devices)])
        gathered = lax.dynamic_update_index_in_dim(gathered, block, (me + devices - shift) % devices, 0)
    return gathered


def sum_over_ctx(first, second):
    devices = lax.axis_size("ctx")
    if devices != 2:
        return lax.psum((first, second), "ctx")
    both = jnp.stack([first, second])
    total = both + lax.ppermute(both, "ctx", [(0, 1), (1, 0)])
    return total[0], total[1]


def on_device(hidden_in, weight, clip_upper, clip_lower, filters, gate, target):
    shards = lax.axis_size("fsdp")
    width = hidden_in.shape[-1]
    local_rows = hidden_in.reshape(-1, width)
    length = local_rows.shape[0]
    rows, columns = weight.shape
    values = weight.astype(jnp.float32)
    quant = soft_clip(values, clip_upper, clip_lower).astype(jnp.bfloat16)
    pieces, quant = rows_of_block(local_rows, shards, rows, quant)
    me = lax.axis_index("fsdp")
    sums = []
    for piece, _ in pieces:
        count = piece.shape[1]
        flat = piece.reshape(shards * count, rows)
        partial = jnp.dot(flat, quant, preferred_element_type=jnp.float32).reshape(shards, count, columns)
        sums.append(reduce_partial(partial, me))
    if len(pieces) == 1:
        proj, mine = sums[0], pieces[0][0]
    else:
        first = pieces[0][1] == 0
        proj = jnp.where(first, jnp.concatenate(sums, axis=0), jnp.concatenate(sums[::-1], axis=0))
        halves = [piece for piece, _ in pieces]
        mine = jnp.where(first, jnp.concatenate(halves, axis=1), jnp.concatenate(halves[::-1], axis=1))
    proj = proj.astype(jnp.bfloat16)
    inputs = mine.reshape(shards * length, rows)

    taps = jnp.repeat(filters, CGROUP, axis=0).T
    pad = FILT - 1
    previous = from_behind(proj[length - pad :], "ctx", 1)
    upcoming = from_behind(proj[:pad], "ctx", -1)
    gates_in = gate.reshape(length, columns)
    wanted_in = target.reshape(length, columns)
    gates_next = from_behind(gates_in[:pad], "ctx", -1)
    wanted_next = from_behind(wanted_in[:pad], "ctx", -1)
    padded = jnp.concatenate([previous, proj, upcoming], axis=0).astype(jnp.float32)
    extent = length + pad
    conv = jnp.zeros((extent, columns), jnp.float32)
    for tap in range(FILT):
        conv = conv + taps[tap] * padded[pad - tap : pad - tap + extent]
    gates = jnp.concatenate([gates_in, gates_next], axis=0).astype(jnp.float32)
    wanted = jnp.concatenate([wanted_in, wanted_next], axis=0).astype(jnp.float32)
    total_tokens = lax.axis_size("fsdp") * lax.axis_size("ctx") * length
    scale = 1024.0 / jnp.sqrt(jnp.float32(total_tokens))
    d_conv = scale * (gates * conv - wanted) * gates
    d_proj = jnp.zeros((length, columns), jnp.float32)
    for tap in range(FILT):
        d_proj = d_proj + taps[tap] * d_conv[tap : tap + length]
    d_proj = d_proj.astype(jnp.bfloat16)

    d_all = ring_gather(d_proj, "fsdp").reshape(shards * length, columns)
    d_clipped = lax.dot_general(
        inputs, d_all, (((0,), (0,)), ((), ())), preferred_element_type=jnp.float32
    )
    grad_up, grad_low = soft_clip_grads(values, clip_upper, clip_lower, d_clipped)
    grad_upper, grad_lower = sum_over_ctx(grad_up, grad_low)
    return (grad_upper, grad_lower)


def solution(mesh):
    return jax.shard_map(
        on_device,
        mesh=mesh,
        in_specs=(
            P(("parts", "fsdp"), "ctx", None, "seq"),
            P("fsdp", "seq"),
            P(("parts", "fsdp"), "seq"),
            P(("parts", "fsdp"), "seq"),
            P("seq", None),
            P(("parts", "fsdp"), "ctx", None, "seq"),
            P(("parts", "fsdp"), "ctx", None, "seq"),
        ),
        out_specs=(P(("parts", "fsdp"), "seq"), P(("parts", "fsdp"), "seq")),
        check_vma=False,
    )
```

```python
import jax
import jax.numpy as jnp
from jax import lax
from jax.sharding import PartitionSpec as P

FILT = 7
CGROUP = 16


def from_behind(value, axis, by):
    devices = lax.axis_size(axis)
    pairs = [(i, i + by) for i in range(devices) if 0 <= i + by < devices]
    return lax.ppermute(value, axis, pairs)


def clip_bounds(values, upper_logit, lower_logit):
    rows = values.shape[0]
    groups = upper_logit.shape[0]
    blocks = values.reshape(groups, rows // groups, values.shape[1])
    amax = jnp.max(jnp.abs(blocks.astype(jnp.bfloat16)), axis=1).astype(jnp.float32) + 1e-06
    upper = jax.nn.sigmoid(upper_logit) * amax
    lower = -jax.nn.sigmoid(lower_logit) * amax
    center = ((upper + lower) * 0.5)[:, None, :]
    radius = ((upper - lower) * 0.5)[:, None, :]
    return blocks, amax, center, radius


def soft_clip(values, upper_logit, lower_logit):
    blocks, _, center, radius = clip_bounds(values, upper_logit, lower_logit)
    clipped = center + radius * jnp.tanh((blocks - center) * (1.0 / radius))
    return clipped.reshape(values.shape)


def soft_clip_grads(values, upper_logit, lower_logit, d_clipped):
    blocks, amax, center, radius = clip_bounds(values, upper_logit, lower_logit)
    z = (blocks - center) * (1.0 / radius)
    t = jnp.tanh(z)
    square = t * t
    slope = t - (1.0 - square) * z
    grouped = d_clipped.reshape(blocks.shape)
    toward_upper = jnp.sum(grouped * (square + slope), axis=1)
    toward_lower = jnp.sum(grouped * (square - slope), axis=1)
    up = jax.nn.sigmoid(upper_logit)
    low = jax.nn.sigmoid(lower_logit)
    grad_up = toward_upper * (0.5 * up * (1.0 - up) * amax)
    grad_low = toward_lower * (-0.5 * low * (1.0 - low) * amax)
    return grad_up, grad_low


def gather_features(local_rows):
    devices = lax.axis_size("seq")
    if devices != 2:
        return lax.all_gather(local_rows, "seq", axis=1, tiled=True)
    other = lax.ppermute(local_rows, "seq", [(0, 1), (1, 0)])
    first = lax.axis_index("seq") == 0
    return jnp.where(
        first,
        jnp.concatenate([local_rows, other], axis=1),
        jnp.concatenate([other, local_rows], axis=1),
    )


def rows_of_block(local_rows, shards, rows, quant):
    devices = lax.axis_size("seq")
    length = local_rows.shape[0]
    if devices != 2 or length % 2:
        features, quant = lax.optimization_barrier((gather_features(local_rows), quant))
        pieces = features.reshape(length, shards, rows).transpose(1, 0, 2)
        return [(lax.all_to_all(pieces, "fsdp", 0, 0), 0)], quant
    half = length // 2
    first = lax.axis_index("seq") == 0
    lower, upper = local_rows[:half], local_rows[half:]
    wanted_by_other = jnp.where(first, upper, lower)
    kept = jnp.where(first, lower, upper)
    other = lax.ppermute(wanted_by_other, "seq", [(0, 1), (1, 0)])
    other, quant = lax.optimization_barrier((other, quant))
    features = jnp.where(
        first, jnp.concatenate([kept, other], axis=1), jnp.concatenate([other, kept], axis=1)
    )
    pieces = features.reshape(half, shards, rows).transpose(1, 0, 2)
    own_half = lax.all_to_all(pieces, "fsdp", 0, 0)
    other_half = lax.ppermute(own_half, "seq", [(0, 1), (1, 0)])
    own_at = jnp.where(first, 0, half)
    return [(own_half, own_at), (other_half, half - own_at)], quant


def reduce_partial(partial, me):
    shards = partial.shape[0]
    received = lax.all_to_all(partial.astype(jnp.float16), "fsdp", 0, 0).astype(jnp.float32)
    others = jnp.where((jnp.arange(shards) == me)[:, None, None], 0.0, received)
    own = lax.dynamic_index_in_dim(partial, me, 0, keepdims=False)
    return own + jnp.sum(others, axis=0)


def ring_gather(value, axis):
    devices = lax.axis_size(axis)
    me = lax.axis_index(axis)
    gathered = jnp.broadcast_to(value[None], (devices,) + value.shape)
    for shift in range(1, devices):
        block = lax.ppermute(value, axis, [(i, (i + shift) % devices) for i in range(devices)])
        gathered = lax.dynamic_update_index_in_dim(gathered, block, (me + devices - shift) % devices, 0)
    return gathered


def sum_over_ctx(first, second):
    devices = lax.axis_size("ctx")
    if devices != 2:
        return lax.psum((first, second), "ctx")
    both = jnp.stack([first, second])
    total = both + lax.ppermute(both, "ctx", [(0, 1), (1, 0)])
    return total[0], total[1]


def on_device(hidden_in, weight, clip_upper, clip_lower, filters, gate, target):
    shards = lax.axis_size("fsdp")
    width = hidden_in.shape[-1]
    local_rows = hidden_in.reshape(-1, width)
    length = local_rows.shape[0]
    rows, columns = weight.shape
    values = weight.astype(jnp.float32)
    quant = soft_clip(values, clip_upper, clip_lower).astype(jnp.bfloat16)
    pieces, quant = rows_of_block(local_rows, shards, rows, quant)
    me = lax.axis_index("fsdp")
    sums = []
    for piece, _ in pieces:
        count = piece.shape[1]
        flat = piece.reshape(shards * count, rows)
        partial = jnp.dot(flat, quant, preferred_element_type=jnp.float32).reshape(shards, count, columns)
        sums.append(reduce_partial(partial, me))
    if len(pieces) == 1:
        proj, mine = sums[0], pieces[0][0]
    else:
        first = pieces[0][1] == 0
        proj = jnp.where(first, jnp.concatenate(sums, axis=0), jnp.concatenate(sums[::-1], axis=0))
        halves = [piece for piece, _ in pieces]
        mine = jnp.where(first, jnp.concatenate(halves, axis=1), jnp.concatenate(halves[::-1], axis=1))
    proj = proj.astype(jnp.bfloat16)
    inputs = mine.reshape(shards * length, rows)

    taps = jnp.repeat(filters, CGROUP, axis=0).T
    pad = FILT - 1
    previous = from_behind(proj[length - pad :], "ctx", 1)
    upcoming = from_behind(proj[:pad], "ctx", -1)
    gates_in = gate.reshape(length, columns)
    wanted_in = target.reshape(length, columns)
    gates_next = from_behind(gates_in[:pad], "ctx", -1)
    wanted_next = from_behind(wanted_in[:pad], "ctx", -1)
    padded = jnp.concatenate([previous, proj, upcoming], axis=0).astype(jnp.float32)
    extent = length + pad
    conv = jnp.zeros((extent, columns), jnp.float32)
    for tap in range(FILT):
        conv = conv + taps[tap] * padded[pad - tap : pad - tap + extent]
    gates = jnp.concatenate([gates_in, gates_next], axis=0).astype(jnp.float32)
    wanted = jnp.concatenate([wanted_in, wanted_next], axis=0).astype(jnp.float32)
    total_tokens = lax.axis_size("fsdp") * lax.axis_size("ctx") * length
    scale = 1024.0 / jnp.sqrt(jnp.float32(total_tokens))
    d_conv = scale * (gates * conv - wanted) * gates
    d_proj = jnp.zeros((length, columns), jnp.float32)
    for tap in range(FILT):
        d_proj = d_proj + taps[tap] * d_conv[tap : tap + length]
    d_proj = d_proj.astype(jnp.bfloat16)

    d_all = ring_gather(d_proj, "fsdp").reshape(shards * length, columns)
    d_clipped = lax.dot_general(
        inputs, d_all, (((0,), (0,)), ((), ())), preferred_element_type=jnp.float32
    )
    grad_up, grad_low = soft_clip_grads(values, clip_upper, clip_lower, d_clipped)
    grad_upper, grad_lower = sum_over_ctx(grad_up, grad_low)
    return (grad_upper, grad_lower)


def solution(mesh):
    return jax.shard_map(
        on_device,
        mesh=mesh,
        in_specs=(
            P(("parts", "fsdp"), "ctx", None, "seq"),
            P("fsdp", "seq"),
            P(("parts", "fsdp"), "seq"),
            P(("parts", "fsdp"), "seq"),
            P("seq", None),
            P(("parts", "fsdp"), "ctx", None, "seq"),
            P(("parts", "fsdp"), "ctx", None, "seq"),
        ),
        out_specs=(P(("parts", "fsdp"), "seq"), P(("parts", "fsdp"), "seq")),
        check_vma=False,
    )
```

```python
import jax
import jax.numpy as jnp
from jax import lax
from jax.sharding import PartitionSpec as P

FILT = 7
CGROUP = 16


def from_behind(value, axis, by):
    devices = lax.axis_size(axis)
    pairs = [(i, i + by) for i in range(devices) if 0 <= i + by < devices]
    return lax.ppermute(value, axis, pairs)


def clip_bounds(values, upper_logit, lower_logit):
    rows = values.shape[0]
    groups = upper_logit.shape[0]
    blocks = values.reshape(groups, rows // groups, values.shape[1])
    amax = jnp.max(jnp.abs(blocks.astype(jnp.bfloat16)), axis=1).astype(jnp.float32) + 1e-06
    upper = jax.nn.sigmoid(upper_logit) * amax
    lower = -jax.nn.sigmoid(lower_logit) * amax
    center = ((upper + lower) * 0.5)[:, None, :]
    radius = ((upper - lower) * 0.5)[:, None, :]
    return blocks, amax, center, radius


def soft_clip(values, upper_logit, lower_logit):
    blocks, _, center, radius = clip_bounds(values, upper_logit, lower_logit)
    clipped = center + radius * jnp.tanh((blocks - center) * (1.0 / radius))
    return clipped.reshape(values.shape)


def soft_clip_grads(values, upper_logit, lower_logit, d_clipped):
    blocks, amax, center, radius = clip_bounds(values, upper_logit, lower_logit)
    z = (blocks - center) * (1.0 / radius)
    t = jnp.tanh(z)
    square = t * t
    slope = t - (1.0 - square) * z
    grouped = d_clipped.reshape(blocks.shape)
    toward_upper = jnp.sum(grouped * (square + slope), axis=1)
    toward_lower = jnp.sum(grouped * (square - slope), axis=1)
    up = jax.nn.sigmoid(upper_logit)
    low = jax.nn.sigmoid(lower_logit)
    grad_up = toward_upper * (0.5 * up * (1.0 - up) * amax)
    grad_low = toward_lower * (-0.5 * low * (1.0 - low) * amax)
    return grad_up, grad_low


def gather_features(local_rows):
    devices = lax.axis_size("seq")
    if devices != 2:
        return lax.all_gather(local_rows, "seq", axis=1, tiled=True)
    other = lax.ppermute(local_rows, "seq", [(0, 1), (1, 0)])
    first = lax.axis_index("seq") == 0
    return jnp.where(
        first,
        jnp.concatenate([local_rows, other], axis=1),
        jnp.concatenate([other, local_rows], axis=1),
    )


def rows_of_block(local_rows, shards, rows, quant):
    devices = lax.axis_size("seq")
    length = local_rows.shape[0]
    if devices != 2 or length % 2:
        features, quant = lax.optimization_barrier((gather_features(local_rows), quant))
        pieces = features.reshape(length, shards, rows).transpose(1, 0, 2)
        return [(lax.all_to_all(pieces, "fsdp", 0, 0), 0)], quant
    half = length // 2
    first = lax.axis_index("seq") == 0
    lower, upper = local_rows[:half], local_rows[half:]
    wanted_by_other = jnp.where(first, upper, lower)
    other = lax.ppermute(wanted_by_other, "seq", [(0, 1), (1, 0)])
    other, quant = lax.optimization_barrier((other, quant))
    features = jnp.where(
        first, jnp.concatenate([lower, other], axis=1), jnp.concatenate([other, upper], axis=1)
    )
    pieces = features.reshape(half, shards, rows).transpose(1, 0, 2)
    own_half = lax.all_to_all(pieces, "fsdp", 0, 0)
    other_half = lax.ppermute(own_half, "seq", [(0, 1), (1, 0)])
    own_at = jnp.where(first, 0, half)
    return [(own_half, own_at), (other_half, half - own_at)], quant


def reduce_partial(partial, me):
    shards = partial.shape[0]
    received = lax.all_to_all(partial.astype(jnp.float16), "fsdp", 0, 0).astype(jnp.float32)
    others = jnp.where((jnp.arange(shards) == me)[:, None, None], 0.0, received)
    own = lax.dynamic_index_in_dim(partial, me, 0, keepdims=False)
    return own + jnp.sum(others, axis=0)


def ring_gather(value, axis):
    devices = lax.axis_size(axis)
    me = lax.axis_index(axis)
    gathered = jnp.broadcast_to(value[None], (devices,) + value.shape)
    for shift in range(1, devices):
        block = lax.ppermute(value, axis, [(i, (i + shift) % devices) for i in range(devices)])
        gathered = lax.dynamic_update_index_in_dim(gathered, block, (me + devices - shift) % devices, 0)
    return gathered


def sum_over_ctx(first, second):
    devices = lax.axis_size("ctx")
    if devices != 2:
        return lax.psum((first, second), "ctx")
    both = jnp.stack([first, second])
    total = both + lax.ppermute(both, "ctx", [(0, 1), (1, 0)])
    return total[0], total[1]


def on_device(hidden_in, weight, clip_upper, clip_lower, filters, gate, target):
    shards = lax.axis_size("fsdp")
    width = hidden_in.shape[-1]
    local_rows = hidden_in.reshape(-1, width)
    length = local_rows.shape[0]
    rows, columns = weight.shape
    values = weight.astype(jnp.float32)
    quant = soft_clip(values, clip_upper, clip_lower).astype(jnp.bfloat16)
    pieces, quant = rows_of_block(local_rows, shards, rows, quant)
    me = lax.axis_index("fsdp")
    sums = []
    for piece, _ in pieces:
        count = piece.shape[1]
        flat = piece.reshape(shards * count, rows)
        partial = jnp.dot(flat, quant, preferred_element_type=jnp.float32).reshape(shards, count, columns)
        sums.append(reduce_partial(partial, me))
    if len(pieces) == 1:
        proj, mine = sums[0], pieces[0][0]
    else:
        first = pieces[0][1] == 0
        proj = jnp.where(first, jnp.concatenate(sums, axis=0), jnp.concatenate(sums[::-1], axis=0))
        halves = [piece for piece, _ in pieces]
        mine = jnp.where(first, jnp.concatenate(halves, axis=1), jnp.concatenate(halves[::-1], axis=1))
    proj = proj.astype(jnp.bfloat16)
    inputs = mine.reshape(shards * length, rows)

    taps = jnp.repeat(filters, CGROUP, axis=0).T
    pad = FILT - 1
    previous = from_behind(proj[length - pad :], "ctx", 1)
    upcoming = from_behind(proj[:pad], "ctx", -1)
    gates_in = gate.reshape(length, columns)
    wanted_in = target.reshape(length, columns)
    gates_next = from_behind(gates_in[:pad], "ctx", -1)
    wanted_next = from_behind(wanted_in[:pad], "ctx", -1)
    padded = jnp.concatenate([previous, proj, upcoming], axis=0).astype(jnp.float32)
    extent = length + pad
    conv = jnp.zeros((extent, columns), jnp.float32)
    for tap in range(FILT):
        conv = conv + taps[tap] * padded[pad - tap : pad - tap + extent]
    gates = jnp.concatenate([gates_in, gates_next], axis=0).astype(jnp.float32)
    wanted = jnp.concatenate([wanted_in, wanted_next], axis=0).astype(jnp.float32)
    total_tokens = lax.axis_size("fsdp") * lax.axis_size("ctx") * length
    scale = 1024.0 / jnp.sqrt(jnp.float32(total_tokens))
    d_conv = scale * (gates * conv - wanted) * gates
    d_proj = jnp.zeros((length, columns), jnp.float32)
    for tap in range(FILT):
        d_proj = d_proj + taps[tap] * d_conv[tap : tap + length]
    d_proj = d_proj.astype(jnp.bfloat16)

    d_all = ring_gather(d_proj, "fsdp").reshape(shards * length, columns)
    d_clipped = lax.dot_general(
        inputs, d_all, (((0,), (0,)), ((), ())), preferred_element_type=jnp.float32
    )
    grad_up, grad_low = soft_clip_grads(values, clip_upper, clip_lower, d_clipped)
    grad_upper, grad_lower = sum_over_ctx(grad_up, grad_low)
    return (grad_upper, grad_lower)


def solution(mesh):
    return jax.shard_map(
        on_device,
        mesh=mesh,
        in_specs=(
            P(("parts", "fsdp"), "ctx", None, "seq"),
            P("fsdp", "seq"),
            P(("parts", "fsdp"), "seq"),
            P(("parts", "fsdp"), "seq"),
            P("seq", None),
            P(("parts", "fsdp"), "ctx", None, "seq"),
            P(("parts", "fsdp"), "ctx", None, "seq"),
        ),
        out_specs=(P(("parts", "fsdp"), "seq"), P(("parts", "fsdp"), "seq")),
        check_vma=False,
    )
```

```python
import jax
import jax.numpy as jnp
from jax import lax
from jax.sharding import PartitionSpec as P

FILT = 7
CGROUP = 16


def from_behind(value, axis, by):
    devices = lax.axis_size(axis)
    pairs = [(i, i + by) for i in range(devices) if 0 <= i + by < devices]
    return lax.ppermute(value, axis, pairs)


def clip_bounds(values, upper_logit, lower_logit):
    rows = values.shape[0]
    groups = upper_logit.shape[0]
    blocks = values.reshape(groups, rows // groups, values.shape[1])
    amax = jnp.max(jnp.abs(blocks.astype(jnp.bfloat16)), axis=1).astype(jnp.float32) + 1e-06
    upper = jax.nn.sigmoid(upper_logit) * amax
    lower = -jax.nn.sigmoid(lower_logit) * amax
    center = ((upper + lower) * 0.5)[:, None, :]
    radius = ((upper - lower) * 0.5)[:, None, :]
    return blocks, amax, center, radius


def soft_clip(values, upper_logit, lower_logit):
    blocks, _, center, radius = clip_bounds(values, upper_logit, lower_logit)
    clipped = center + radius * jnp.tanh((blocks - center) * (1.0 / radius))
    return clipped.reshape(values.shape)


def soft_clip_grads(values, upper_logit, lower_logit, d_clipped):
    blocks, amax, center, radius = clip_bounds(values, upper_logit, lower_logit)
    z = (blocks - center) * (1.0 / radius)
    t = jnp.tanh(z)
    square = t * t
    slope = t - (1.0 - square) * z
    grouped = d_clipped.reshape(blocks.shape)
    toward_upper = jnp.sum(grouped * (square + slope), axis=1)
    toward_lower = jnp.sum(grouped * (square - slope), axis=1)
    up = jax.nn.sigmoid(upper_logit)
    low = jax.nn.sigmoid(lower_logit)
    grad_up = toward_upper * (0.5 * up * (1.0 - up) * amax)
    grad_low = toward_lower * (-0.5 * low * (1.0 - low) * amax)
    return grad_up, grad_low


def gather_features(local_rows):
    devices = lax.axis_size("seq")
    if devices != 2:
        return lax.all_gather(local_rows, "seq", axis=1, tiled=True)
    other = lax.ppermute(local_rows, "seq", [(0, 1), (1, 0)])
    first = lax.axis_index("seq") == 0
    return jnp.where(
        first,
        jnp.concatenate([local_rows, other], axis=1),
        jnp.concatenate([other, local_rows], axis=1),
    )


def rows_of_block(local_rows, shards, rows, quant):
    devices = lax.axis_size("seq")
    length = local_rows.shape[0]
    if devices != 2 or length % 2:
        features, quant = lax.optimization_barrier((gather_features(local_rows), quant))
        pieces = features.reshape(length, shards, rows).transpose(1, 0, 2)
        return [(lax.all_to_all(pieces, "fsdp", 0, 0), 0)], quant
    half = length // 2
    first = lax.axis_index("seq") == 0
    lower, upper = local_rows[:half], local_rows[half:]
    wanted_by_other = jnp.where(first, upper, lower)
    kept = jnp.where(first, lower, upper)
    other = lax.ppermute(wanted_by_other, "seq", [(0, 1), (1, 0)])
    other, quant = lax.optimization_barrier((other, quant))
    features = jnp.where(
        first, jnp.concatenate([kept, other], axis=1), jnp.concatenate([other, kept], axis=1)
    )
    pieces = features.reshape(half, shards, rows).transpose(1, 0, 2)
    own_half = lax.all_to_all(pieces, "fsdp", 0, 0)
    other_half = lax.ppermute(own_half, "seq", [(0, 1), (1, 0)])
    own_at = jnp.where(first, 0, half)
    return [(own_half, own_at), (other_half, half - own_at)], quant


def reduce_partial(partial, me):
    shards = partial.shape[0]
    received = lax.all_to_all(partial.astype(jnp.float16), "fsdp", 0, 0)
    others = jnp.where((jnp.arange(shards) == me)[:, None, None], 0.0, received).astype(jnp.float32)
    own = lax.dynamic_index_in_dim(partial, me, 0, keepdims=False)
    return own + jnp.sum(others, axis=0)


def ring_gather(value, axis):
    devices = lax.axis_size(axis)
    me = lax.axis_index(axis)
    gathered = jnp.broadcast_to(value[None], (devices,) + value.shape)
    for shift in range(1, devices):
        block = lax.ppermute(value, axis, [(i, (i + shift) % devices) for i in range(devices)])
        gathered = lax.dynamic_update_index_in_dim(gathered, block, (me + devices - shift) % devices, 0)
    return gathered


def sum_over_ctx(first, second):
    devices = lax.axis_size("ctx")
    if devices != 2:
        return lax.psum((first, second), "ctx")
    both = jnp.stack([first, second])
    total = both + lax.ppermute(both, "ctx", [(0, 1), (1, 0)])
    return total[0], total[1]


def on_device(hidden_in, weight, clip_upper, clip_lower, filters, gate, target):
    shards = lax.axis_size("fsdp")
    width = hidden_in.shape[-1]
    local_rows = hidden_in.reshape(-1, width)
    length = local_rows.shape[0]
    rows, columns = weight.shape
    values = weight.astype(jnp.float32)
    quant = soft_clip(values, clip_upper, clip_lower).astype(jnp.bfloat16)
    pieces, quant = rows_of_block(local_rows, shards, rows, quant)
    me = lax.axis_index("fsdp")
    sums = []
    for piece, _ in pieces:
        count = piece.shape[1]
        flat = piece.reshape(shards * count, rows)
        partial = jnp.dot(flat, quant, preferred_element_type=jnp.float32).reshape(shards, count, columns)
        sums.append(reduce_partial(partial, me))
    if len(pieces) == 1:
        proj, mine = sums[0], pieces[0][0]
    else:
        first = pieces[0][1] == 0
        proj = jnp.where(first, jnp.concatenate(sums, axis=0), jnp.concatenate(sums[::-1], axis=0))
        halves = [piece for piece, _ in pieces]
        mine = jnp.where(first, jnp.concatenate(halves, axis=1), jnp.concatenate(halves[::-1], axis=1))
    proj = proj.astype(jnp.bfloat16)
    inputs = mine.reshape(shards * length, rows)

    taps = jnp.repeat(filters, CGROUP, axis=0).T
    pad = FILT - 1
    previous = from_behind(proj[length - pad :], "ctx", 1)
    upcoming = from_behind(proj[:pad], "ctx", -1)
    gates_in = gate.reshape(length, columns)
    wanted_in = target.reshape(length, columns)
    gates_next = from_behind(gates_in[:pad], "ctx", -1)
    wanted_next = from_behind(wanted_in[:pad], "ctx", -1)
    padded = jnp.concatenate([previous, proj, upcoming], axis=0).astype(jnp.float32)
    extent = length + pad
    conv = jnp.zeros((extent, columns), jnp.float32)
    for tap in range(FILT):
        conv = conv + taps[tap] * padded[pad - tap : pad - tap + extent]
    gates = jnp.concatenate([gates_in, gates_next], axis=0).astype(jnp.float32)
    wanted = jnp.concatenate([wanted_in, wanted_next], axis=0).astype(jnp.float32)
    total_tokens = lax.axis_size("fsdp") * lax.axis_size("ctx") * length
    scale = 1024.0 / jnp.sqrt(jnp.float32(total_tokens))
    d_conv = scale * (gates * conv - wanted) * gates
    d_proj = jnp.zeros((length, columns), jnp.float32)
    for tap in range(FILT):
        d_proj = d_proj + taps[tap] * d_conv[tap : tap + length]
    d_proj = d_proj.astype(jnp.bfloat16)

    d_all = ring_gather(d_proj, "fsdp").reshape(shards * length, columns)
    d_clipped = lax.dot_general(
        inputs, d_all, (((0,), (0,)), ((), ())), preferred_element_type=jnp.float32
    )
    grad_up, grad_low = soft_clip_grads(values, clip_upper, clip_lower, d_clipped)
    grad_upper, grad_lower = sum_over_ctx(grad_up, grad_low)
    return (grad_upper, grad_lower)


def solution(mesh):
    return jax.shard_map(
        on_device,
        mesh=mesh,
        in_specs=(
            P(("parts", "fsdp"), "ctx", None, "seq"),
            P("fsdp", "seq"),
            P(("parts", "fsdp"), "seq"),
            P(("parts", "fsdp"), "seq"),
            P("seq", None),
            P(("parts", "fsdp"), "ctx", None, "seq"),
            P(("parts", "fsdp"), "ctx", None, "seq"),
        ),
        out_specs=(P(("parts", "fsdp"), "seq"), P(("parts", "fsdp"), "seq")),
        check_vma=False,
    )
```

```python
import jax
import jax.numpy as jnp
from jax import lax
from jax.sharding import PartitionSpec as P

FILT = 7
CGROUP = 16


def from_behind(value, axis, by):
    devices = lax.axis_size(axis)
    pairs = [(i, i + by) for i in range(devices) if 0 <= i + by < devices]
    return lax.ppermute(value, axis, pairs)


def clip_bounds(values, upper_logit, lower_logit):
    rows = values.shape[0]
    groups = upper_logit.shape[0]
    blocks = values.reshape(groups, rows // groups, values.shape[1])
    amax = jnp.max(jnp.abs(blocks.astype(jnp.bfloat16)), axis=1).astype(jnp.float32) + 1e-06
    upper = jax.nn.sigmoid(upper_logit) * amax
    lower = -jax.nn.sigmoid(lower_logit) * amax
    center = ((upper + lower) * 0.5)[:, None, :]
    radius = ((upper - lower) * 0.5)[:, None, :]
    return blocks, amax, center, radius


def soft_clip(values, upper_logit, lower_logit):
    blocks, _, center, radius = clip_bounds(values, upper_logit, lower_logit)
    clipped = center + radius * jnp.tanh((blocks - center) * (1.0 / radius))
    return clipped.reshape(values.shape)


def soft_clip_grads(values, upper_logit, lower_logit, d_clipped):
    blocks, amax, center, radius = clip_bounds(values, upper_logit, lower_logit)
    z = (blocks - center) * (1.0 / radius)
    t = jnp.tanh(z)
    square = t * t
    slope = t - (1.0 - square) * z
    grouped = d_clipped.reshape(blocks.shape)
    toward_upper = jnp.sum(grouped * (square + slope), axis=1)
    toward_lower = jnp.sum(grouped * (square - slope), axis=1)
    up = jax.nn.sigmoid(upper_logit)
    low = jax.nn.sigmoid(lower_logit)
    grad_up = toward_upper * (0.5 * up * (1.0 - up) * amax)
    grad_low = toward_lower * (-0.5 * low * (1.0 - low) * amax)
    return grad_up, grad_low


def gather_features(local_rows):
    devices = lax.axis_size("seq")
    if devices != 2:
        return lax.all_gather(local_rows, "seq", axis=1, tiled=True)
    other = lax.ppermute(local_rows, "seq", [(0, 1), (1, 0)])
    first = lax.axis_index("seq") == 0
    return jnp.where(
        first,
        jnp.concatenate([local_rows, other], axis=1),
        jnp.concatenate([other, local_rows], axis=1),
    )


def rows_of_block(local_rows, shards, rows, quant):
    devices = lax.axis_size("seq")
    length = local_rows.shape[0]
    if devices != 2 or length % 2:
        features, quant = lax.optimization_barrier((gather_features(local_rows), quant))
        pieces = features.reshape(length, shards, rows).transpose(1, 0, 2)
        return [(lax.all_to_all(pieces, "fsdp", 0, 0), 0)], quant
    half = length // 2
    first = lax.axis_index("seq") == 0
    lower, upper = local_rows[:half], local_rows[half:]
    wanted_by_other = jnp.where(first, upper, lower)
    kept = jnp.where(first, lower, upper)
    other = lax.ppermute(wanted_by_other, "seq", [(0, 1), (1, 0)])
    other, quant = lax.optimization_barrier((other, quant))
    features = jnp.where(
        first, jnp.concatenate([kept, other], axis=1), jnp.concatenate([other, kept], axis=1)
    )
    pieces = features.reshape(half, shards, rows).transpose(1, 0, 2)
    own_half = lax.all_to_all(pieces, "fsdp", 0, 0)
    other_half = lax.ppermute(own_half, "seq", [(0, 1), (1, 0)])
    own_at = jnp.where(first, 0, half)
    return [(own_half, own_at), (other_half, half - own_at)], quant


def reduce_partial(partial, me):
    shards = partial.shape[0]
    received = lax.all_to_all(partial.astype(jnp.float16), "fsdp", 0, 0).astype(jnp.float32)
    others = jnp.where((jnp.arange(shards) == me)[:, None, None], 0.0, received)
    own = lax.dynamic_index_in_dim(partial, me, 0, keepdims=False)
    return own + jnp.sum(others, axis=0)


def ring_gather(value, axis):
    devices = lax.axis_size(axis)
    me = lax.axis_index(axis)
    gathered = jnp.broadcast_to(value[None], (devices,) + value.shape)
    for shift in range(1, devices):
        block = lax.ppermute(value, axis, [(i, (i + shift) % devices) for i in range(devices)])
        gathered = lax.dynamic_update_index_in_dim(gathered, block, (me + devices - shift) % devices, 0)
    return gathered


def sum_over_ctx(first, second):
    devices = lax.axis_size("ctx")
    if devices != 2:
        return lax.psum((first, second), "ctx")
    both = jnp.stack([first, second])
    total = both + lax.ppermute(both, "ctx", [(0, 1), (1, 0)])
    return total[0], total[1]


def on_device(hidden_in, weight, clip_upper, clip_lower, filters, gate, target):
    shards = lax.axis_size("fsdp")
    width = hidden_in.shape[-1]
    local_rows = hidden_in.reshape(-1, width)
    length = local_rows.shape[0]
    rows, columns = weight.shape
    values = weight.astype(jnp.float32)
    quant = soft_clip(values, clip_upper, clip_lower).astype(jnp.bfloat16)
    pieces, quant = rows_of_block(local_rows, shards, rows, quant)
    me = lax.axis_index("fsdp")
    sums = []
    for piece, _ in pieces:
        count = piece.shape[1]
        flat = piece.reshape(shards * count, rows)
        partial = jnp.dot(flat, quant, preferred_element_type=jnp.float32).reshape(shards, count, columns)
        sums.append(reduce_partial(partial, me))
    if len(pieces) == 1:
        proj, mine = sums[0], pieces[0][0]
    else:
        first = pieces[0][1] == 0
        proj = jnp.where(first, jnp.concatenate(sums, axis=0), jnp.concatenate(sums[::-1], axis=0))
        halves = [piece for piece, _ in pieces]
        mine = jnp.where(first, jnp.concatenate(halves, axis=1), jnp.concatenate(halves[::-1], axis=1))
    proj = proj.astype(jnp.bfloat16)
    inputs = mine.reshape(shards * length, rows)

    taps = jnp.repeat(filters, CGROUP, axis=0).T
    pad = FILT - 1
    previous = from_behind(proj[length - pad :], "ctx", 1)
    gates_in = gate.reshape(length, columns)
    wanted_in = target.reshape(length, columns)
    ahead = from_behind(jnp.stack([proj[:pad], gates_in[:pad].astype(proj.dtype), wanted_in[:pad].astype(proj.dtype)]), "ctx", -1)
    upcoming, gates_next, wanted_next = ahead[0], ahead[1], ahead[2]
    padded = jnp.concatenate([previous, proj, upcoming], axis=0).astype(jnp.float32)
    extent = length + pad
    conv = jnp.zeros((extent, columns), jnp.float32)
    for tap in range(FILT):
        conv = conv + taps[tap] * padded[pad - tap : pad - tap + extent]
    gates = jnp.concatenate([gates_in, gates_next], axis=0).astype(jnp.float32)
    wanted = jnp.concatenate([wanted_in, wanted_next], axis=0).astype(jnp.float32)
    total_tokens = lax.axis_size("fsdp") * lax.axis_size("ctx") * length
    scale = 1024.0 / jnp.sqrt(jnp.float32(total_tokens))
    d_conv = scale * (gates * conv - wanted) * gates
    d_proj = jnp.zeros((length, columns), jnp.float32)
    for tap in range(FILT):
        d_proj = d_proj + taps[tap] * d_conv[tap : tap + length]
    d_proj = d_proj.astype(jnp.bfloat16)

    d_all = ring_gather(d_proj, "fsdp").reshape(shards * length, columns)
    d_clipped = lax.dot_general(
        inputs, d_all, (((0,), (0,)), ((), ())), preferred_element_type=jnp.float32
    )
    grad_up, grad_low = soft_clip_grads(values, clip_upper, clip_lower, d_clipped)
    grad_upper, grad_lower = sum_over_ctx(grad_up, grad_low)
    return (grad_upper, grad_lower)


def solution(mesh):
    return jax.shard_map(
        on_device,
        mesh=mesh,
        in_specs=(
            P(("parts", "fsdp"), "ctx", None, "seq"),
            P("fsdp", "seq"),
            P(("parts", "fsdp"), "seq"),
            P(("parts", "fsdp"), "seq"),
            P("seq", None),
            P(("parts", "fsdp"), "ctx", None, "seq"),
            P(("parts", "fsdp"), "ctx", None, "seq"),
        ),
        out_specs=(P(("parts", "fsdp"), "seq"), P(("parts", "fsdp"), "seq")),
        check_vma=False,
    )
```
